32 devices in a mesh: strip: 8 (over z, y), blk: 2 (over x), dp: 2 (over core).
Axes of the slice: x: 2, y: 2, z: 4, core: 2. Of those that a mesh axis runs over, the one named last changes fastest.
Arguments:
- fields: bfloat16 [4, 256, 128, 128], P('dp', 'blk', 'strip'), may hold values from -6 to 6
- cotangent: bfloat16 [4, 256, 128, 128], P('dp', 'blk', 'strip'), may hold values from -6 to 6
- kernel_one: float32 [9, 128], replicated, may hold values from -2 to 2
- weight_one: bfloat16 [128, 128], replicated, may hold values from -0.5 to 0.5
- kernel_two: float32 [9, 128], replicated, may hold values from -2 to 2
- weight_two: bfloat16 [128, 128], replicated, may hold values from -0.5 to 0.5
- seam_flags: int32 [2, 8], replicated, may hold values from 0 to 1, as said below
Outputs:
- grad_fields: bfloat16 [4, 256, 128, 128], P('dp', 'blk', 'strip')
- grad_kernel_one: float32 [9, 128], replicated
- grad_weight_one: float32 [128, 128], replicated
- grad_kernel_two: float32 [9, 128], replicated
- grad_weight_two: float32 [128, 128], replicated
The draws below stay inside these ranges and needn't reach their ends.
Inputs may be any that keep to these rules, and one draw needn't show every extreme that they name: seam_flags[q, s] is 0 unless s is a multiple of 2 (a seam between two faces); at such a seam it is 1 where the row order reverses.
All inputs are finite; a program needn't handle non-finite values.
Results may differ from the reference program's by a relative error of at most 0.0056.
Values may be sent and summed in bfloat16 or wider, within the bound.
No kernel may reach another device: no remote copies, remote signals or barrier semaphores. Data moves between devices by JAX's collectives and lax.ppermute only.
A program may use at most 128 MiB of HBM per device.

```python
import jax
import jax.numpy as jnp
from jax import lax

CH = 128
ROW_DEV = 128
COL_DEV = 16
BATCH = 4
ROWS = 256
CYCLE = 128
FACE_CYCLES = 2
STRIPS = 8
FACE_STRIPS = 2
N_STRIP = 8
N_BLK = 2


def draw_seam_flags(key, part):
    face_bits = jax.random.randint(key, (FACE_CYCLES, 4), 0, 2).astype(jnp.int32)
    face_bits = face_bits.at[0, 0].set(1)
    face_bits = face_bits.at[0, 1].set(0)
    columns = jnp.arange(STRIPS)
    on_seam = columns % FACE_STRIPS == 0
    face_of = (columns // FACE_STRIPS).astype(jnp.int32)
    picked = face_bits[:, face_of]
    return jnp.where(on_seam[None, :], picked, 0).astype(jnp.int32)


def level_of(own_key, shape, split, least, top_value):
    def one(dim, shards_of):
        heights = jax.random.uniform(jax.random.fold_in(jax.random.fold_in(own_key, 6), dim), (shards_of,), jnp.float32, least / len(split), top_value / len(split))
        return jnp.repeat(jnp.exp(heights), shape[dim] // shards_of).reshape((-1,) + (1,) * (len(shape) - dim - 1))

    loudness = one(*split[0])
    for cut in split[1:]:
        loudness = loudness * one(*cut)
    return loudness


def bell_draw(rng, shape, spread, reach, split=(), held_as=jnp.bfloat16):
    result = spread * jax.random.normal(rng, shape, jnp.float32)
    if split:
        result = result * level_of(rng, shape, split, -0.22, 0.18)
    return jnp.clip(result, -reach, reach).astype(held_as)


def setup_inputs(seed: int = 0) -> dict:
    arg_keys = jax.random.split(jax.random.key(seed), 8)
    return {
        "fields": bell_draw(arg_keys[0], (BATCH, ROWS, CYCLE, CH), 1.0, 6.0, ((0, 2), (1, 2), (2, 8))),
        "cotangent": bell_draw(arg_keys[1], (BATCH, ROWS, CYCLE, CH), 1.0, 6.0, ((0, 2), (1, 2), (2, 8))),
        "kernel_one": bell_draw(arg_keys[2], (9, CH), 9 ** -0.5, 2.0, (), jnp.float32),
        "weight_one": bell_draw(arg_keys[3], (CH, CH), CH ** -0.5, 0.5),
        "kernel_two": bell_draw(arg_keys[4], (9, CH), 9 ** -0.5, 2.0, (), jnp.float32),
        "weight_two": bell_draw(arg_keys[5], (CH, CH), CH ** -0.5, 0.5),
        "seam_flags": draw_seam_flags(jax.random.fold_in(arg_keys[7], 71), 0),
    }


def extend(values, seam_flags, margin):
    blocks = values.reshape(N_BLK, ROW_DEV, N_STRIP, COL_DEV, CH)
    from_left = jnp.roll(blocks[:, :, :, COL_DEV - margin:], 1, axis=2)
    from_right = jnp.roll(blocks[:, :, :, :margin], -1, axis=2)
    flag_left = (seam_flags == 1)[:, None, :, None, None]
    flag_right = (jnp.roll(seam_flags, -1, axis=1) == 1)[:, None, :, None, None]
    from_left = jnp.where(flag_left, from_left[:, ::-1], from_left)
    from_right = jnp.where(flag_right, from_right[:, ::-1], from_right)
    widened = jnp.concatenate([from_left, blocks, from_right], axis=3)
    widened = widened.reshape(ROWS, N_STRIP, COL_DEV + 2 * margin, CH)
    zero_rows = jnp.zeros((margin,) + widened.shape[1:], widened.dtype)
    return jnp.concatenate([zero_rows, widened, zero_rows], axis=0)

def depthwise(widened, kernel, margin):
    summed = jnp.zeros((ROWS, N_STRIP, COL_DEV, CH), jnp.float32)
    for tap_row in range(3):
        for tap_col in range(3):
            tap_slice = widened[tap_row * margin:tap_row * margin + ROWS, :, tap_col * margin:tap_col * margin + COL_DEV]
            summed = summed + tap_slice.astype(jnp.float32) * kernel[3 * tap_row + tap_col]
    return summed.reshape(ROWS, CYCLE, CH)

def pointwise(act, weight):
    return jnp.dot(act.reshape(-1, CH), weight, preferred_element_type=jnp.float32).reshape(act.shape)

def block_back(values, pre_val, act, grad_out, seam_flags, kernel, weight, margin):
    flat_grad = grad_out.reshape(-1, CH)
    d_weight = jnp.dot(act.reshape(-1, CH).T, flat_grad, preferred_element_type=jnp.float32)
    d_act = jnp.dot(flat_grad, weight.T, preferred_element_type=jnp.float32).reshape(pre_val.shape)
    logistic = jax.nn.sigmoid(pre_val)
    d_pre = d_act * logistic * (1.0 + pre_val * (1.0 - logistic))

    def conv_map(tensor, kern):
        return depthwise(extend(tensor, seam_flags, margin), kern, margin)
    unused, pull_back = jax.vjp(conv_map, values.astype(jnp.float32), kernel)
    d_values, d_kernel = pull_back(d_pre)
    grad_in = (grad_out.astype(jnp.float32) + d_values).astype(jnp.bfloat16)
    return (grad_in, d_kernel, d_weight)

def reference(fields, cotangent, kernel_one, weight_one, kernel_two, weight_two, seam_flags):

    def per_item(running, inputs):
        sample, grad_sample = inputs
        pre_one = depthwise(extend(sample, seam_flags, 1), kernel_one, 1)
        act_one = jax.nn.silu(pre_one).astype(jnp.bfloat16)
        hidden = (sample.astype(jnp.float32) + pointwise(act_one, weight_one)).astype(jnp.bfloat16)
        pre_two = depthwise(extend(hidden, seam_flags, 2), kernel_two, 2)
        act_two = jax.nn.silu(pre_two).astype(jnp.bfloat16)
        grad_hidden, dk_two, dw_two = block_back(hidden, pre_two, act_two, grad_sample, seam_flags, kernel_two, weight_two, 2)
        grad_input, dk_one, dw_one = block_back(sample, pre_one, act_one, grad_hidden, seam_flags, kernel_one, weight_one, 1)
        fresh = (dk_one, dw_one, dk_two, dw_two)
        return (tuple((older + newer for older, newer in zip(running, fresh))), grad_input)
    start = (jnp.zeros((9, CH), jnp.float32), jnp.zeros((CH, CH), jnp.float32), jnp.zeros((9, CH), jnp.float32), jnp.zeros((CH, CH), jnp.float32))
    totals, grad_fields = lax.scan(per_item, start, (fields, cotangent))
    factor = float(BATCH * ROWS * CYCLE) ** (-0.5)
    return (grad_fields, totals[0] * factor, totals[1] * factor, totals[2] * factor, totals[3] * factor)
```

```python
import jax
import jax.numpy as jnp
from jax import lax
from jax.sharding import PartitionSpec as P

COL_DEV = 16


def tree_sum(value, axes):
    sizes = [lax.axis_size(axis) for axis in axes]
    count = 1
    for size in sizes:
        count *= size
    if count & (count - 1):
        return lax.psum(value, axes)
    bit = 1
    while bit < count:
        pairs = [(i, i ^ bit) for i in range(count)]
        value = value + lax.ppermute(value, axes, pairs)
        bit *= 2
    return value


def packed_sum(parts, axes, reducer):
    rows = [part.shape[0] for part in parts]
    summed = reducer(jnp.concatenate(parts, axis=0), axes)
    out, start = [], 0
    for count in rows:
        out.append(summed[start : start + count])
        start += count
    return out


def with_halo(shard, sides, width, wrap):
    for axis, dim in sides:
        count, length = (lax.axis_size(axis), shard.shape[dim])
        up = [(i, (i + 1) % count) for i in range(count if wrap else count - 1)]
        down = [(j, i) for i, j in up]
        last = lax.slice_in_dim(shard, length - width, length, axis=dim)
        first = lax.slice_in_dim(shard, 0, width, axis=dim)
        before = lax.ppermute(last, axis, up)
        after = lax.ppermute(first, axis, down)
        shard = jnp.concatenate([before, shard, after], axis=dim)
    return shard


def seam_bits(seam_flags, local_strips):
    circle_idx = lax.axis_index("blk")
    strip_idx = lax.axis_index("strip")
    strip_total = seam_flags.shape[1]
    circle_flags = lax.dynamic_index_in_dim(seam_flags, circle_idx, 0, keepdims=False)
    global_strip = strip_idx * local_strips + jnp.arange(local_strips, dtype=jnp.int32)
    next_strip = (global_strip + 1) % strip_total
    left_flip = jnp.take(circle_flags, global_strip) == 1
    right_flip = jnp.take(circle_flags, next_strip) == 1
    return (left_flip[None, None, :, None, None], right_flip[None, None, :, None, None])


def extend(values, margin, seams):
    batch_size, row_count, col_total, channels = values.shape
    local_strips = col_total // COL_DEV
    strips = values.reshape(batch_size, row_count, local_strips, COL_DEV, channels)
    rim_cols = jnp.concatenate(
        [strips[:, :, 0, :margin], strips[:, :, local_strips - 1, COL_DEV - margin :]], axis=2
    )
    padded = with_halo(rim_cols, (("strip", 2),), margin, True)
    halo_left = padded[:, :, :margin][:, :, None]
    halo_right = padded[:, :, 3 * margin :][:, :, None]
    from_left = jnp.concatenate(
        [halo_left, strips[:, :, : local_strips - 1, COL_DEV - margin :]], axis=2
    )
    from_right = jnp.concatenate([strips[:, :, 1:, :margin], halo_right], axis=2)
    from_left = jnp.where(seams[0], from_left[:, ::-1], from_left)
    from_right = jnp.where(seams[1], from_right[:, ::-1], from_right)
    widened = jnp.concatenate([from_left, strips, from_right], axis=3)
    rim_rows = jnp.concatenate([widened[:, :margin], widened[:, row_count - margin :]], axis=1)
    padded_rows = with_halo(rim_rows, (("blk", 1),), margin, False)
    return jnp.concatenate([padded_rows[:, :margin], widened, padded_rows[:, 3 * margin :]], axis=1)


def depthwise(widened, kernel, margin, row_count):
    batch_size, unused_rows, local_strips, unused_cols, channels = widened.shape
    summed = jnp.zeros((batch_size, row_count, local_strips, COL_DEV, channels), jnp.float32)
    for tap_row in range(3):
        for tap_col in range(3):
            tap_slice = widened[
                :,
                tap_row * margin : tap_row * margin + row_count,
                :,
                tap_col * margin : tap_col * margin + COL_DEV,
            ]
            summed = summed + tap_slice * kernel[3 * tap_row + tap_col]
    return summed.reshape(batch_size, row_count, local_strips * COL_DEV, channels)


def conv_back(widened, kernel, grad_pre, margin):
    batch_size, row_count, col_total, channels = grad_pre.shape
    local_strips = col_total // COL_DEV
    grad_strips = grad_pre.reshape(batch_size, row_count, local_strips, COL_DEV, channels)
    grad_wide = jnp.zeros(widened.shape, jnp.float32)
    tap_sums = []
    for tap_row in range(3):
        for tap_col in range(3):
            row_start = tap_row * margin
            col_start = tap_col * margin
            tap_slice = widened[
                :, row_start : row_start + row_count, :, col_start : col_start + COL_DEV
            ]
            tap_sums.append(jnp.sum(tap_slice * grad_strips, axis=(0, 1, 2, 3)))
            placed = jnp.pad(
                kernel[3 * tap_row + tap_col] * grad_strips,
                (
                    (0, 0),
                    (row_start, 2 * margin - row_start),
                    (0, 0),
                    (col_start, 2 * margin - col_start),
                    (0, 0),
                ),
            )
            grad_wide = grad_wide + placed
    return (jnp.stack(tap_sums), grad_wide)


def fold_back(grad_wide, margin, seams):
    batch_size, wide_rows, local_strips, wide_cols, channels = grad_wide.shape
    row_count = wide_rows - 2 * margin
    rim_rows = jnp.concatenate([grad_wide[:, :margin], grad_wide[:, wide_rows - margin :]], axis=1)
    padded = with_halo(rim_rows.astype(jnp.bfloat16), (("blk", 1),), margin, False).astype(
        rim_rows.dtype
    )
    core_rows = grad_wide[:, margin : wide_rows - margin]
    no_pad = (0, 0)
    core_rows = core_rows + jnp.pad(
        padded[:, :margin], (no_pad, (0, row_count - margin), no_pad, no_pad, no_pad)
    )
    core_rows = core_rows + jnp.pad(
        padded[:, 3 * margin :], (no_pad, (row_count - margin, 0), no_pad, no_pad, no_pad)
    )
    left_part = core_rows[:, :, :, :margin]
    right_part = core_rows[:, :, :, wide_cols - margin :]
    left_part = jnp.where(seams[0], left_part[:, ::-1], left_part)
    right_part = jnp.where(seams[1], right_part[:, ::-1], right_part)
    rim_cols = jnp.concatenate([left_part[:, :, 0], right_part[:, :, local_strips - 1]], axis=2)
    padded_cols = with_halo(rim_cols.astype(jnp.bfloat16), (("strip", 2),), margin, True).astype(
        rim_cols.dtype
    )
    from_left_dev = padded_cols[:, :, :margin][:, :, None]
    from_right_dev = padded_cols[:, :, 3 * margin :][:, :, None]
    add_first = jnp.concatenate([from_left_dev, right_part[:, :, : local_strips - 1]], axis=2)
    add_last = jnp.concatenate([left_part[:, :, 1:], from_right_dev], axis=2)
    inner_cols = core_rows[:, :, :, margin : wide_cols - margin]
    inner_cols = inner_cols + jnp.pad(
        add_first, (no_pad, no_pad, no_pad, (0, COL_DEV - margin), no_pad)
    )
    inner_cols = inner_cols + jnp.pad(
        add_last, (no_pad, no_pad, no_pad, (COL_DEV - margin, 0), no_pad)
    )
    return inner_cols.reshape(batch_size, row_count, local_strips * COL_DEV, channels)


def pointwise(act, weight):
    channels = act.shape[-1]
    flat_act = act.reshape(-1, channels)
    return jnp.dot(flat_act, weight, preferred_element_type=jnp.float32).reshape(act.shape)


def block_back(widened, pre_val, act, grad_out, kernel, weight, margin, seams):
    channels = act.shape[-1]
    flat_grad = grad_out.reshape(-1, channels)
    d_weight = lax.dot_general(
        act.reshape(-1, channels),
        flat_grad,
        (((0,), (0,)), ((), ())),
        preferred_element_type=jnp.float32,
    )
    d_act = lax.dot_general(
        flat_grad, weight, (((1,), (1,)), ((), ())), preferred_element_type=jnp.float32
    ).reshape(pre_val.shape)
    logistic = jax.nn.sigmoid(pre_val)
    d_pre = d_act * logistic * (1.0 + pre_val * (1.0 - logistic))
    d_kernel, grad_wide = conv_back(widened, kernel, d_pre, margin)
    d_values = fold_back(grad_wide, margin, seams)
    grad_in = (grad_out.astype(jnp.float32) + d_values).astype(jnp.bfloat16)
    return (grad_in, d_kernel, d_weight)


def shards(fields, cotangent, kernel_one, weight_one, kernel_two, weight_two, seam_flags):
    batch_size, row_count, col_count, channels = fields.shape
    seams = seam_bits(seam_flags, col_count // COL_DEV)
    cells_all = (
        batch_size
        * row_count
        * col_count
        * lax.axis_size("strip")
        * lax.axis_size("blk")
        * lax.axis_size("dp")
    )
    factor = float(cells_all) ** (-0.5)
    wide_one = extend(fields, 1, seams)
    pre_one = depthwise(wide_one, kernel_one, 1, row_count)
    act_one = jax.nn.silu(pre_one).astype(jnp.bfloat16)
    hidden = (fields.astype(jnp.float32) + pointwise(act_one, weight_one)).astype(jnp.bfloat16)
    wide_two = extend(hidden, 2, seams)
    pre_two = depthwise(wide_two, kernel_two, 2, row_count)
    act_two = jax.nn.silu(pre_two).astype(jnp.bfloat16)
    grad_hidden, dk_two, dw_two = block_back(
        wide_two, pre_two, act_two, cotangent, kernel_two, weight_two, 2, seams
    )
    grad_fields, dk_one, dw_one = block_back(
        wide_one, pre_one, act_one, grad_hidden, kernel_one, weight_one, 1, seams
    )
    dk_one, dw_one, dk_two, dw_two = packed_sum(
        (dk_one, dw_one, dk_two, dw_two), ("strip", "blk", "dp"), tree_sum
    )
    return (grad_fields, dk_one * factor, dw_one * factor, dk_two * factor, dw_two * factor)


def solution(mesh):
    return jax.shard_map(
        shards,
        mesh=mesh,
        in_specs=(
            P("dp", "blk", "strip", None),
            P("dp", "blk", "strip", None),
            P(),
            P(),
            P(),
            P(),
            P(),
        ),
        out_specs=(P("dp", "blk", "strip", None), P(), P(), P(), P()),
        check_vma=False,
    )
```

```python
import jax
import jax.numpy as jnp
from jax import lax
from jax.sharding import PartitionSpec as P
from jax.experimental import pallas as pl
from jax.experimental.pallas import tpu as pltpu
import functools

COL_DEV = 16
ROW_BLOCK = 8


def conv_back_body(margin, wide_ref, gpad_ref, k_ref, gw_ref, dk_ref):
    batch, wide_rows, wide_cols, channels = wide_ref.shape
    row_count = wide_rows - 2 * margin
    col_count = wide_cols - 2 * margin
    taps = [(a, b) for a in range(3) for b in range(3)]
    kern = k_ref[...]
    sums = [jnp.zeros((col_count, channels), jnp.float32) for _ in taps]
    for item in range(batch):

        def tap_step(step, sums):
            r0 = pl.multiple_of(step * ROW_BLOCK, ROW_BLOCK)
            grad = gpad_ref[item, pl.ds(r0 + 2 * margin, ROW_BLOCK), pl.ds(2 * margin, col_count), :]
            out = []
            for t, (a, b) in enumerate(taps):
                seen = wide_ref[item, pl.ds(r0 + a * margin, ROW_BLOCK), pl.ds(b * margin, col_count), :]
                out.append(sums[t] + jnp.sum(seen * grad, axis=0))
            return out

        sums = lax.fori_loop(0, row_count // ROW_BLOCK, tap_step, sums)

        def wide_step(step, carry):
            r0 = step * ROW_BLOCK
            total = jnp.zeros((ROW_BLOCK, wide_cols, channels), jnp.float32)
            for t, (a, b) in enumerate(taps):
                part = gpad_ref[
                    item,
                    pl.ds(r0 + 2 * margin - a * margin, ROW_BLOCK),
                    pl.ds(2 * margin - b * margin, wide_cols),
                    :,
                ]
                total = total + part * kern[t][None, None, :]
            gw_ref[item, pl.ds(r0, ROW_BLOCK), :, :] = total
            return carry

        full = wide_rows // ROW_BLOCK
        lax.fori_loop(0, full, wide_step, 0)
        rest = wide_rows - full * ROW_BLOCK
        if rest:
            r0 = full * ROW_BLOCK
            total = jnp.zeros((rest, wide_cols, channels), jnp.float32)
            for t, (a, b) in enumerate(taps):
                part = gpad_ref[
                    item,
                    pl.ds(r0 + 2 * margin - a * margin, rest),
                    pl.ds(2 * margin - b * margin, wide_cols),
                    :,
                ]
                total = total + part * kern[t][None, None, :]
            gw_ref[item, pl.ds(r0, rest), :, :] = total
    dk_ref[...] = jnp.concatenate([jnp.sum(s, axis=0, keepdims=True) for s in sums], axis=0)


def conv_back_kernel(wide, grad, kernel, margin):
    batch, wide_rows, wide_cols, channels = wide.shape
    gpad = jnp.pad(grad, ((0, 0), (2 * margin, 2 * margin), (2 * margin, 2 * margin), (0, 0)))
    elems = batch * wide_rows * wide_cols * channels
    return pl.pallas_call(
        functools.partial(conv_back_body, margin),
        out_shape=(
            jax.ShapeDtypeStruct(wide.shape, jnp.float32),
            jax.ShapeDtypeStruct((9, channels), jnp.float32),
        ),
        in_specs=[pl.BlockSpec(memory_space=pltpu.VMEM)] * 3,
        out_specs=(pl.BlockSpec(memory_space=pltpu.VMEM), pl.BlockSpec(memory_space=pltpu.VMEM)),
        compiler_params=pltpu.CompilerParams(vmem_limit_bytes=48 * 1024 * 1024),
        cost_estimate=pl.CostEstimate(flops=36 * elems, bytes_accessed=12 * elems, transcendentals=0),
    )(wide.astype(jnp.float32), gpad, kernel)


def tree_sum(value, axes):
    sizes = [lax.axis_size(axis) for axis in axes]
    count = 1
    for size in sizes:
        count *= size
    if count & (count - 1):
        return lax.psum(value, axes)
    bit = 1
    while bit < count:
        pairs = [(i, i ^ bit) for i in range(count)]
        value = value + lax.ppermute(value, axes, pairs)
        bit *= 2
    return value


def packed_sum(parts, axes, reducer):
    rows = [part.shape[0] for part in parts]
    summed = reducer(jnp.concatenate(parts, axis=0), axes)
    out, start = [], 0
    for count in rows:
        out.append(summed[start : start + count])
        start += count
    return out


def swap_halo(shard, axis, dim, width, length):
    last = lax.slice_in_dim(shard, length - width, length, axis=dim)
    first = lax.slice_in_dim(shard, 0, width, axis=dim)
    upper = lax.axis_index(axis) == 0
    sent = jnp.where(upper, last, first)
    got = lax.ppermute(sent, axis, [(0, 1), (1, 0)])
    zeros = jnp.zeros_like(got)
    before = jnp.where(upper, zeros, got)
    after = jnp.where(upper, got, zeros)
    return jnp.concatenate([before, shard, after], axis=dim)


def with_halo(shard, sides, width, wrap):
    for axis, dim in sides:
        count, length = (lax.axis_size(axis), shard.shape[dim])
        if count == 2 and not wrap:
            shard = swap_halo(shard, axis, dim, width, length)
            continue
        up = [(i, (i + 1) % count) for i in range(count if wrap else count - 1)]
        down = [(j, i) for i, j in up]
        last = lax.slice_in_dim(shard, length - width, length, axis=dim)
        first = lax.slice_in_dim(shard, 0, width, axis=dim)
        before = lax.ppermute(last, axis, up)
        after = lax.ppermute(first, axis, down)
        shard = jnp.concatenate([before, shard, after], axis=dim)
    return shard


def seam_bits(seam_flags, local_strips):
    circle_idx = lax.axis_index("blk")
    strip_idx = lax.axis_index("strip")
    strip_total = seam_flags.shape[1]
    circle_flags = lax.dynamic_index_in_dim(seam_flags, circle_idx, 0, keepdims=False)
    global_strip = strip_idx * local_strips + jnp.arange(local_strips, dtype=jnp.int32)
    next_strip = (global_strip + 1) % strip_total
    left_flip = jnp.take(circle_flags, global_strip) == 1
    right_flip = jnp.take(circle_flags, next_strip) == 1
    return (left_flip[None, None, :, None, None], right_flip[None, None, :, None, None])


def extend(values, margin, seams):
    batch_size, row_count, col_total, channels = values.shape
    local_strips = col_total // COL_DEV
    strips = values.reshape(batch_size, row_count, local_strips, COL_DEV, channels)
    rim_cols = jnp.concatenate(
        [strips[:, :, 0, :margin], strips[:, :, local_strips - 1, COL_DEV - margin :]], axis=2
    )
    padded = with_halo(rim_cols, (("strip", 2),), margin, True)
    halo_left = padded[:, :, :margin][:, :, None]
    halo_right = padded[:, :, 3 * margin :][:, :, None]
    from_left = jnp.concatenate(
        [halo_left, strips[:, :, : local_strips - 1, COL_DEV - margin :]], axis=2
    )
    from_right = jnp.concatenate([strips[:, :, 1:, :margin], halo_right], axis=2)
    from_left = jnp.where(seams[0], from_left[:, ::-1], from_left)
    from_right = jnp.where(seams[1], from_right[:, ::-1], from_right)
    widened = jnp.concatenate([from_left, strips, from_right], axis=3)
    rim_rows = jnp.concatenate([widened[:, :margin], widened[:, row_count - margin :]], axis=1)
    padded_rows = with_halo(rim_rows, (("blk", 1),), margin, False)
    return jnp.concatenate([padded_rows[:, :margin], widened, padded_rows[:, 3 * margin :]], axis=1)


def depthwise(widened, kernel, margin, row_count):
    batch_size, unused_rows, local_strips, unused_cols, channels = widened.shape
    summed = jnp.zeros((batch_size, row_count, local_strips, COL_DEV, channels), jnp.float32)
    for tap_row in range(3):
        for tap_col in range(3):
            tap_slice = widened[
                :,
                tap_row * margin : tap_row * margin + row_count,
                :,
                tap_col * margin : tap_col * margin + COL_DEV,
            ]
            summed = summed + tap_slice * kernel[3 * tap_row + tap_col]
    return summed.reshape(batch_size, row_count, local_strips * COL_DEV, channels)


def conv_back(widened, kernel, grad_pre, margin):
    batch_size, row_count, col_total, channels = grad_pre.shape
    unused, wide_rows, local_strips, wide_cols, unused_ch = widened.shape
    flat_wide = jnp.swapaxes(widened, 1, 2).reshape(-1, wide_rows, wide_cols, channels)
    grad_strips = grad_pre.reshape(batch_size, row_count, local_strips, COL_DEV, channels)
    flat_grad = jnp.swapaxes(grad_strips, 1, 2).reshape(-1, row_count, COL_DEV, channels)
    grad_wide, tap_sums = conv_back_kernel(flat_wide, flat_grad, kernel, margin)
    grad_wide = grad_wide.reshape(batch_size, local_strips, wide_rows, wide_cols, channels)
    return (tap_sums, jnp.swapaxes(grad_wide, 1, 2))


def fold_back(grad_wide, margin, seams):
    batch_size, wide_rows, local_strips, wide_cols, channels = grad_wide.shape
    row_count = wide_rows - 2 * margin
    rim_rows = jnp.concatenate([grad_wide[:, :margin], grad_wide[:, wide_rows - margin :]], axis=1)
    padded = with_halo(rim_rows.astype(jnp.bfloat16), (("blk", 1),), margin, False).astype(
        rim_rows.dtype
    )
    core_rows = grad_wide[:, margin : wide_rows - margin]
    no_pad = (0, 0)
    core_rows = core_rows + jnp.pad(
        padded[:, :margin], (no_pad, (0, row_count - margin), no_pad, no_pad, no_pad)
    )
    core_rows = core_rows + jnp.pad(
        padded[:, 3 * margin :], (no_pad, (row_count - margin, 0), no_pad, no_pad, no_pad)
    )
    left_part = core_rows[:, :, :, :margin]
    right_part = core_rows[:, :, :, wide_cols - margin :]
    left_part = jnp.where(seams[0], left_part[:, ::-1], left_part)
    right_part = jnp.where(seams[1], right_part[:, ::-1], right_part)
    rim_cols = jnp.concatenate([left_part[:, :, 0], right_part[:, :, local_strips - 1]], axis=2)
    padded_cols = with_halo(rim_cols.astype(jnp.bfloat16), (("strip", 2),), margin, True).astype(
        rim_cols.dtype
    )
    from_left_dev = padded_cols[:, :, :margin][:, :, None]
    from_right_dev = padded_cols[:, :, 3 * margin :][:, :, None]
    add_first = jnp.concatenate([from_left_dev, right_part[:, :, : local_strips - 1]], axis=2)
    add_last = jnp.concatenate([left_part[:, :, 1:], from_right_dev], axis=2)
    inner_cols = core_rows[:, :, :, margin : wide_cols - margin]
    inner_cols = inner_cols + jnp.pad(
        add_first, (no_pad, no_pad, no_pad, (0, COL_DEV - margin), no_pad)
    )
    inner_cols = inner_cols + jnp.pad(
        add_last, (no_pad, no_pad, no_pad, (COL_DEV - margin, 0), no_pad)
    )
    return inner_cols.reshape(batch_size, row_count, local_strips * COL_DEV, channels)


def pointwise(act, weight):
    channels = act.shape[-1]
    flat_act = act.reshape(-1, channels)
    return jnp.dot(flat_act, weight, preferred_element_type=jnp.float32).reshape(act.shape)


def block_back(widened, pre_val, act, grad_out, kernel, weight, margin, seams):
    channels = act.shape[-1]
    flat_grad = grad_out.reshape(-1, channels)
    d_weight = lax.dot_general(
        act.reshape(-1, channels),
        flat_grad,
        (((0,), (0,)), ((), ())),
        preferred_element_type=jnp.float32,
    )
    d_act = lax.dot_general(
        flat_grad, weight, (((1,), (1,)), ((), ())), preferred_element_type=jnp.float32
    ).reshape(pre_val.shape)
    logistic = jax.nn.sigmoid(pre_val)
    d_pre = d_act * logistic * (1.0 + pre_val * (1.0 - logistic))
    d_kernel, grad_wide = conv_back(widened, kernel, d_pre, margin)
    d_values = fold_back(grad_wide, margin, seams)
    grad_in = (grad_out.astype(jnp.float32) + d_values).astype(jnp.bfloat16)
    return (grad_in, d_kernel, d_weight)


def shards(fields, cotangent, kernel_one, weight_one, kernel_two, weight_two, seam_flags):
    batch_size, row_count, col_count, channels = fields.shape
    seams = seam_bits(seam_flags, col_count // COL_DEV)
    cells_all = (
        batch_size
        * row_count
        * col_count
        * lax.axis_size("strip")
        * lax.axis_size("blk")
        * lax.axis_size("dp")
    )
    factor = float(cells_all) ** (-0.5)
    wide_one = extend(fields, 1, seams)
    pre_one = depthwise(wide_one, kernel_one, 1, row_count)
    act_one = jax.nn.silu(pre_one).astype(jnp.bfloat16)
    hidden = (fields.astype(jnp.float32) + pointwise(act_one, weight_one)).astype(jnp.bfloat16)
    wide_two = extend(hidden, 2, seams)
    pre_two = depthwise(wide_two, kernel_two, 2, row_count)
    act_two = jax.nn.silu(pre_two).astype(jnp.bfloat16)
    grad_hidden, dk_two, dw_two = block_back(
        wide_two, pre_two, act_two, cotangent, kernel_two, weight_two, 2, seams
    )
    grad_fields, dk_one, dw_one = block_back(
        wide_one, pre_one, act_one, grad_hidden, kernel_one, weight_one, 1, seams
    )
    dk_one, dw_one, dk_two, dw_two = packed_sum(
        (dk_one, dw_one, dk_two, dw_two), ("strip", "blk", "dp"), tree_sum
    )
    return (grad_fields, dk_one * factor, dw_one * factor, dk_two * factor, dw_two * factor)


def solution(mesh):
    return jax.shard_map(
        shards,
        mesh=mesh,
        in_specs=(
            P("dp", "blk", "strip", None),
            P("dp", "blk", "strip", None),
            P(),
            P(),
            P(),
            P(),
            P(),
        ),
        out_specs=(P("dp", "blk", "strip", None), P(), P(), P(), P()),
        check_vma=False,
    )
```

```python
import jax
import jax.numpy as jnp
from jax import lax
from jax.sharding import PartitionSpec as P
from jax.experimental import pallas as pl
from jax.experimental.pallas import tpu as pltpu
import functools

COL_DEV = 16
ROW_BLOCK = 8


def conv_back_body(margin, wide_ref, grad_ref, k_ref, gw_ref, dk_ref, gpad_ref):
    batch, wide_rows, wide_cols, channels = wide_ref.shape
    row_count = wide_rows - 2 * margin
    col_count = wide_cols - 2 * margin
    taps = [(a, b) for a in range(3) for b in range(3)]
    kern = k_ref[...]
    sums = [jnp.zeros((col_count, channels), jnp.float32) for _ in taps]
    for item in range(batch):
        gpad_ref[...] = jnp.zeros(gpad_ref.shape, jnp.float32)

        def fill_step(step, carry):
            r0 = pl.multiple_of(step * ROW_BLOCK, ROW_BLOCK)
            gpad_ref[pl.ds(r0 + 2 * margin, ROW_BLOCK), pl.ds(2 * margin, col_count), :] = grad_ref[
                item, pl.ds(r0, ROW_BLOCK)
            ]
            return carry

        lax.fori_loop(0, row_count // ROW_BLOCK, fill_step, 0)

        def tap_step(step, sums):
            r0 = pl.multiple_of(step * ROW_BLOCK, ROW_BLOCK)
            grad = grad_ref[item, pl.ds(r0, ROW_BLOCK)]
            out = []
            for t, (a, b) in enumerate(taps):
                seen = wide_ref[item, pl.ds(r0 + a * margin, ROW_BLOCK), pl.ds(b * margin, col_count), :]
                out.append(sums[t] + jnp.sum(seen * grad, axis=0))
            return out

        sums = lax.fori_loop(0, row_count // ROW_BLOCK, tap_step, sums)

        def wide_step(step, carry):
            r0 = step * ROW_BLOCK
            total = jnp.zeros((ROW_BLOCK, wide_cols, channels), jnp.float32)
            for t, (a, b) in enumerate(taps):
                part = gpad_ref[
                    pl.ds(r0 + 2 * margin - a * margin, ROW_BLOCK),
                    pl.ds(2 * margin - b * margin, wide_cols),
                    :,
                ]
                total = total + part * kern[t][None, None, :]
            gw_ref[item, pl.ds(r0, ROW_BLOCK), :, :] = total
            return carry

        full = wide_rows // ROW_BLOCK
        lax.fori_loop(0, full, wide_step, 0)
        rest = wide_rows - full * ROW_BLOCK
        if rest:
            r0 = full * ROW_BLOCK
            total = jnp.zeros((rest, wide_cols, channels), jnp.float32)
            for t, (a, b) in enumerate(taps):
                part = gpad_ref[
                    pl.ds(r0 + 2 * margin - a * margin, rest),
                    pl.ds(2 * margin - b * margin, wide_cols),
                    :,
                ]
                total = total + part * kern[t][None, None, :]
            gw_ref[item, pl.ds(r0, rest), :, :] = total
    dk_ref[...] = jnp.concatenate([jnp.sum(s, axis=0, keepdims=True) for s in sums], axis=0)


def conv_back_kernel(wide, grad, kernel, margin):
    batch, wide_rows, wide_cols, channels = wide.shape
    elems = batch * wide_rows * wide_cols * channels
    pad_rows = grad.shape[1] + 4 * margin
    pad_cols = -(-(grad.shape[2] + 4 * margin) // 8) * 8
    return pl.pallas_call(
        functools.partial(conv_back_body, margin),
        out_shape=(
            jax.ShapeDtypeStruct(wide.shape, jnp.float32),
            jax.ShapeDtypeStruct((9, channels), jnp.float32),
        ),
        in_specs=[pl.BlockSpec(memory_space=pltpu.VMEM)] * 3,
        out_specs=(pl.BlockSpec(memory_space=pltpu.VMEM), pl.BlockSpec(memory_space=pltpu.VMEM)),
        scratch_shapes=[pltpu.VMEM((pad_rows, pad_cols, channels), jnp.float32)],
        compiler_params=pltpu.CompilerParams(vmem_limit_bytes=48 * 1024 * 1024),
        cost_estimate=pl.CostEstimate(flops=36 * elems, bytes_accessed=12 * elems, transcendentals=0),
    )(wide.astype(jnp.float32), grad, kernel)


def tree_sum(value, axes):
    sizes = [lax.axis_size(axis) for axis in axes]
    count = 1
    for size in sizes:
        count *= size
    if count & (count - 1):
        return lax.psum(value, axes)
    bit = 1
    while bit < count:
        pairs = [(i, i ^ bit) for i in range(count)]
        value = value + lax.ppermute(value, axes, pairs)
        bit *= 2
    return value


def packed_sum(parts, axes, reducer):
    rows = [part.shape[0] for part in parts]
    summed = reducer(jnp.concatenate(parts, axis=0), axes)
    out, start = [], 0
    for count in rows:
        out.append(summed[start : start + count])
        start += count
    return out


def swap_halo(shard, axis, dim, width, length):
    last = lax.slice_in_dim(shard, length - width, length, axis=dim)
    first = lax.slice_in_dim(shard, 0, width, axis=dim)
    upper = lax.axis_index(axis) == 0
    sent = jnp.where(upper, last, first)
    got = lax.ppermute(sent, axis, [(0, 1), (1, 0)])
    zeros = jnp.zeros_like(got)
    before = jnp.where(upper, zeros, got)
    after = jnp.where(upper, got, zeros)
    return jnp.concatenate([before, shard, after], axis=dim)


def with_halo(shard, sides, width, wrap):
    for axis, dim in sides:
        count, length = (lax.axis_size(axis), shard.shape[dim])
        if count == 2 and not wrap:
            shard = swap_halo(shard, axis, dim, width, length)
            continue
        up = [(i, (i + 1) % count) for i in range(count if wrap else count - 1)]
        down = [(j, i) for i, j in up]
        last = lax.slice_in_dim(shard, length - width, length, axis=dim)
        first = lax.slice_in_dim(shard, 0, width, axis=dim)
        before = lax.ppermute(last, axis, up)
        after = lax.ppermute(first, axis, down)
        shard = jnp.concatenate([before, shard, after], axis=dim)
    return shard


def seam_bits(seam_flags, local_strips):
    circle_idx = lax.axis_index("blk")
    strip_idx = lax.axis_index("strip")
    strip_total = seam_flags.shape[1]
    circle_flags = lax.dynamic_index_in_dim(seam_flags, circle_idx, 0, keepdims=False)
    global_strip = strip_idx * local_strips + jnp.arange(local_strips, dtype=jnp.int32)
    next_strip = (global_strip + 1) % strip_total
    left_flip = jnp.take(circle_flags, global_strip) == 1
    right_flip = jnp.take(circle_flags, next_strip) == 1
    return (left_flip[None, None, :, None, None], right_flip[None, None, :, None, None])


def extend(values, margin, seams):
    batch_size, row_count, col_total, channels = values.shape
    local_strips = col_total // COL_DEV
    strips = values.reshape(batch_size, row_count, local_strips, COL_DEV, channels)
    rim_cols = jnp.concatenate(
        [strips[:, :, 0, :margin], strips[:, :, local_strips - 1, COL_DEV - margin :]], axis=2
    )
    padded = with_halo(rim_cols, (("strip", 2),), margin, True)
    halo_left = padded[:, :, :margin][:, :, None]
    halo_right = padded[:, :, 3 * margin :][:, :, None]
    from_left = jnp.concatenate(
        [halo_left, strips[:, :, : local_strips - 1, COL_DEV - margin :]], axis=2
    )
    from_right = jnp.concatenate([strips[:, :, 1:, :margin], halo_right], axis=2)
    from_left = jnp.where(seams[0], from_left[:, ::-1], from_left)
    from_right = jnp.where(seams[1], from_right[:, ::-1], from_right)
    widened = jnp.concatenate([from_left, strips, from_right], axis=3)
    rim_rows = jnp.concatenate([widened[:, :margin], widened[:, row_count - margin :]], axis=1)
    padded_rows = with_halo(rim_rows, (("blk", 1),), margin, False)
    return jnp.concatenate([padded_rows[:, :margin], widened, padded_rows[:, 3 * margin :]], axis=1)


def depthwise(widened, kernel, margin, row_count):
    batch_size, unused_rows, local_strips, unused_cols, channels = widened.shape
    summed = jnp.zeros((batch_size, row_count, local_strips, COL_DEV, channels), jnp.float32)
    for tap_row in range(3):
        for tap_col in range(3):
            tap_slice = widened[
                :,
                tap_row * margin : tap_row * margin + row_count,
                :,
                tap_col * margin : tap_col * margin + COL_DEV,
            ]
            summed = summed + tap_slice * kernel[3 * tap_row + tap_col]
    return summed.reshape(batch_size, row_count, local_strips * COL_DEV, channels)


def conv_back(widened, kernel, grad_pre, margin):
    batch_size, row_count, col_total, channels = grad_pre.shape
    unused, wide_rows, local_strips, wide_cols, unused_ch = widened.shape
    flat_wide = jnp.swapaxes(widened, 1, 2).reshape(-1, wide_rows, wide_cols, channels)
    grad_strips = grad_pre.reshape(batch_size, row_count, local_strips, COL_DEV, channels)
    flat_grad = jnp.swapaxes(grad_strips, 1, 2).reshape(-1, row_count, COL_DEV, channels)
    grad_wide, tap_sums = conv_back_kernel(flat_wide, flat_grad, kernel, margin)
    grad_wide = grad_wide.reshape(batch_size, local_strips, wide_rows, wide_cols, channels)
    return (tap_sums, jnp.swapaxes(grad_wide, 1, 2))


def fold_back(grad_wide, margin, seams):
    batch_size, wide_rows, local_strips, wide_cols, channels = grad_wide.shape
    row_count = wide_rows - 2 * margin
    rim_rows = jnp.concatenate([grad_wide[:, :margin], grad_wide[:, wide_rows - margin :]], axis=1)
    padded = with_halo(rim_rows.astype(jnp.bfloat16), (("blk", 1),), margin, False).astype(
        rim_rows.dtype
    )
    core_rows = grad_wide[:, margin : wide_rows - margin]
    no_pad = (0, 0)
    core_rows = core_rows + jnp.pad(
        padded[:, :margin], (no_pad, (0, row_count - margin), no_pad, no_pad, no_pad)
    )
    core_rows = core_rows + jnp.pad(
        padded[:, 3 * margin :], (no_pad, (row_count - margin, 0), no_pad, no_pad, no_pad)
    )
    left_part = core_rows[:, :, :, :margin]
    right_part = core_rows[:, :, :, wide_cols - margin :]
    left_part = jnp.where(seams[0], left_part[:, ::-1], left_part)
    right_part = jnp.where(seams[1], right_part[:, ::-1], right_part)
    rim_cols = jnp.concatenate([left_part[:, :, 0], right_part[:, :, local_strips - 1]], axis=2)
    padded_cols = with_halo(rim_cols.astype(jnp.bfloat16), (("strip", 2),), margin, True).astype(
        rim_cols.dtype
    )
    from_left_dev = padded_cols[:, :, :margin][:, :, None]
    from_right_dev = padded_cols[:, :, 3 * margin :][:, :, None]
    add_first = jnp.concatenate([from_left_dev, right_part[:, :, : local_strips - 1]], axis=2)
    add_last = jnp.concatenate([left_part[:, :, 1:], from_right_dev], axis=2)
    inner_cols = core_rows[:, :, :, margin : wide_cols - margin]
    inner_cols = inner_cols + jnp.pad(
        add_first, (no_pad, no_pad, no_pad, (0, COL_DEV - margin), no_pad)
    )
    inner_cols = inner_cols + jnp.pad(
        add_last, (no_pad, no_pad, no_pad, (COL_DEV - margin, 0), no_pad)
    )
    return inner_cols.reshape(batch_size, row_count, local_strips * COL_DEV, channels)


def pointwise(act, weight):
    channels = act.shape[-1]
    flat_act = act.reshape(-1, channels)
    return jnp.dot(flat_act, weight, preferred_element_type=jnp.float32).reshape(act.shape)


def block_back(widened, pre_val, act, grad_out, kernel, weight, margin, seams):
    channels = act.shape[-1]
    flat_grad = grad_out.reshape(-1, channels)
    d_weight = lax.dot_general(
        act.reshape(-1, channels),
        flat_grad,
        (((0,), (0,)), ((), ())),
        preferred_element_type=jnp.float32,
    )
    d_act = lax.dot_general(
        flat_grad, weight, (((1,), (1,)), ((), ())), preferred_element_type=jnp.float32
    ).reshape(pre_val.shape)
    logistic = jax.nn.sigmoid(pre_val)
    d_pre = d_act * logistic * (1.0 + pre_val * (1.0 - logistic))
    d_kernel, grad_wide = conv_back(widened, kernel, d_pre, margin)
    d_values = fold_back(grad_wide, margin, seams)
    grad_in = (grad_out.astype(jnp.float32) + d_values).astype(jnp.bfloat16)
    return (grad_in, d_kernel, d_weight)


def shards(fields, cotangent, kernel_one, weight_one, kernel_two, weight_two, seam_flags):
    batch_size, row_count, col_count, channels = fields.shape
    seams = seam_bits(seam_flags, col_count // COL_DEV)
    cells_all = (
        batch_size
        * row_count
        * col_count
        * lax.axis_size("strip")
        * lax.axis_size("blk")
        * lax.axis_size("dp")
    )
    factor = float(cells_all) ** (-0.5)
    wide_one = extend(fields, 1, seams).astype(jnp.float32)
    pre_one = depthwise(wide_one, kernel_one, 1, row_count)
    act_one = jax.nn.silu(pre_one).astype(jnp.bfloat16)
    hidden = (fields.astype(jnp.float32) + pointwise(act_one, weight_one)).astype(jnp.bfloat16)
    wide_two = extend(hidden, 2, seams).astype(jnp.float32)
    pre_two = depthwise(wide_two, kernel_two, 2, row_count)
    act_two = jax.nn.silu(pre_two).astype(jnp.bfloat16)
    grad_hidden, dk_two, dw_two = block_back(
        wide_two, pre_two, act_two, cotangent, kernel_two, weight_two, 2, seams
    )
    grad_fields, dk_one, dw_one = block_back(
        wide_one, pre_one, act_one, grad_hidden, kernel_one, weight_one, 1, seams
    )
    dk_one, dw_one, dk_two, dw_two = packed_sum(
        (dk_one, dw_one, dk_two, dw_two), ("strip", "blk", "dp"), tree_sum
    )
    return (grad_fields, dk_one * factor, dw_one * factor, dk_two * factor, dw_two * factor)


def solution(mesh):
    return jax.shard_map(
        shards,
        mesh=mesh,
        in_specs=(
            P("dp", "blk", "strip", None),
            P("dp", "blk", "strip", None),
            P(),
            P(),
            P(),
            P(),
            P(),
        ),
        out_specs=(P("dp", "blk", "strip", None), P(), P(), P(), P()),
        check_vma=False,
    )
```

```python
import jax
import jax.numpy as jnp
from jax import lax
from jax.sharding import PartitionSpec as P
from jax.experimental import pallas as pl
from jax.experimental.pallas import tpu as pltpu
import functools

COL_DEV = 16
ROW_BLOCK = 8


def tap_sum_body(margin, wide_ref, grad_ref, dk_ref):
    batch, wide_rows, wide_cols, channels = wide_ref.shape
    row_count = wide_rows - 2 * margin
    col_count = wide_cols - 2 * margin
    span = ROW_BLOCK + 2 * margin
    sums = [jnp.zeros((col_count, channels), jnp.float32) for _ in range(9)]
    for item in range(batch):

        def tap_step(step, sums):
            r0 = pl.multiple_of(step * ROW_BLOCK, ROW_BLOCK)
            grad = grad_ref[item, pl.ds(r0, ROW_BLOCK)]
            out = list(sums)
            for b in range(3):
                slab = wide_ref[item, pl.ds(r0, span), pl.ds(b * margin, col_count), :]
                for a in range(3):
                    seen = slab[a * margin : a * margin + ROW_BLOCK]
                    out[3 * a + b] = out[3 * a + b] + jnp.sum(seen * grad, axis=0)
            return out

        sums = lax.fori_loop(0, row_count // ROW_BLOCK, tap_step, sums)
    dk_ref[...] = jnp.concatenate([jnp.sum(s, axis=0, keepdims=True) for s in sums], axis=0)


def wide_grad_body(margin, grad_ref, k_ref, gw_ref, gpad_ref):
    batch, wide_rows, wide_cols, channels = gw_ref.shape
    row_count = wide_rows - 2 * margin
    col_count = wide_cols - 2 * margin
    kern = k_ref[...]
    for item in range(batch):
        gpad_ref[...] = jnp.zeros(gpad_ref.shape, jnp.float32)

        def fill_step(step, carry):
            r0 = pl.multiple_of(step * ROW_BLOCK, ROW_BLOCK)
            gpad_ref[pl.ds(r0 + 2 * margin, ROW_BLOCK), pl.ds(2 * margin, col_count), :] = grad_ref[
                item, pl.ds(r0, ROW_BLOCK)
            ]
            return carry

        lax.fori_loop(0, row_count // ROW_BLOCK, fill_step, 0)

        def wide_rows_at(r0, count):
            total = jnp.zeros((count, wide_cols, channels), jnp.float32)
            for b in range(3):
                slab = gpad_ref[pl.ds(r0, count + 2 * margin), pl.ds(2 * margin - b * margin, wide_cols), :]
                for a in range(3):
                    part = slab[2 * margin - a * margin : 2 * margin - a * margin + count]
                    total = total + part * kern[3 * a + b][None, None, :]
            gw_ref[item, pl.ds(r0, count), :, :] = total

        def wide_step(step, carry):
            wide_rows_at(pl.multiple_of(step * ROW_BLOCK, ROW_BLOCK), ROW_BLOCK)
            return carry

        full = wide_rows // ROW_BLOCK
        lax.fori_loop(0, full, wide_step, 0)
        if wide_rows - full * ROW_BLOCK:
            wide_rows_at(full * ROW_BLOCK, wide_rows - full * ROW_BLOCK)


def conv_back_kernel(wide, grad, kernel, margin):
    batch, wide_rows, wide_cols, channels = wide.shape
    elems = batch * wide_rows * wide_cols * channels
    pad_rows = grad.shape[1] + 4 * margin
    pad_cols = -(-(grad.shape[2] + 4 * margin) // 8) * 8
    vmem = pl.BlockSpec(memory_space=pltpu.VMEM)
    params = pltpu.CompilerParams(vmem_limit_bytes=48 * 1024 * 1024)
    grad_wide = pl.pallas_call(
        functools.partial(wide_grad_body, margin),
        out_shape=jax.ShapeDtypeStruct(wide.shape, jnp.float32),
        in_specs=[vmem, vmem],
        out_specs=vmem,
        scratch_shapes=[pltpu.VMEM((pad_rows, pad_cols, channels), jnp.float32)],
        compiler_params=params,
        cost_estimate=pl.CostEstimate(flops=18 * elems, bytes_accessed=8 * elems, transcendentals=0),
    )(grad, kernel)
    tap_sums = pl.pallas_call(
        functools.partial(tap_sum_body, margin),
        out_shape=jax.ShapeDtypeStruct((9, channels), jnp.float32),
        in_specs=[vmem, vmem],
        out_specs=vmem,
        compiler_params=params,
        cost_estimate=pl.CostEstimate(flops=18 * elems, bytes_accessed=8 * elems, transcendentals=0),
    )(wide.astype(jnp.float32), grad)
    return grad_wide, tap_sums


def tree_sum(value, axes):
    sizes = [lax.axis_size(axis) for axis in axes]
    count = 1
    for size in sizes:
        count *= size
    if count & (count - 1):
        return lax.psum(value, axes)
    bit = 1
    while bit < count:
        pairs = [(i, i ^ bit) for i in range(count)]
        value = value + lax.ppermute(value, axes, pairs)
        bit *= 2
    return value


def packed_sum(parts, axes, reducer):
    rows = [part.shape[0] for part in parts]
    summed = reducer(jnp.concatenate(parts, axis=0), axes)
    out, start = [], 0
    for count in rows:
        out.append(summed[start : start + count])
        start += count
    return out


def swap_halo(shard, axis, dim, width, length):
    last = lax.slice_in_dim(shard, length - width, length, axis=dim)
    first = lax.slice_in_dim(shard, 0, width, axis=dim)
    upper = lax.axis_index(axis) == 0
    sent = jnp.where(upper, last, first)
    got = lax.ppermute(sent, axis, [(0, 1), (1, 0)])
    zeros = jnp.zeros_like(got)
    before = jnp.where(upper, zeros, got)
    after = jnp.where(upper, got, zeros)
    return jnp.concatenate([before, shard, after], axis=dim)


def with_halo(shard, sides, width, wrap):
    for axis, dim in sides:
        count, length = (lax.axis_size(axis), shard.shape[dim])
        if count == 2 and not wrap:
            shard = swap_halo(shard, axis, dim, width, length)
            continue
        up = [(i, (i + 1) % count) for i in range(count if wrap else count - 1)]
        down = [(j, i) for i, j in up]
        last = lax.slice_in_dim(shard, length - width, length, axis=dim)
        first = lax.slice_in_dim(shard, 0, width, axis=dim)
        before = lax.ppermute(last, axis, up)
        after = lax.ppermute(first, axis, down)
        shard = jnp.concatenate([before, shard, after], axis=dim)
    return shard


def seam_bits(seam_flags, local_strips):
    circle_idx = lax.axis_index("blk")
    strip_idx = lax.axis_index("strip")
    strip_total = seam_flags.shape[1]
    circle_flags = lax.dynamic_index_in_dim(seam_flags, circle_idx, 0, keepdims=False)
    global_strip = strip_idx * local_strips + jnp.arange(local_strips, dtype=jnp.int32)
    next_strip = (global_strip + 1) % strip_total
    left_flip = jnp.take(circle_flags, global_strip) == 1
    right_flip = jnp.take(circle_flags, next_strip) == 1
    return (left_flip[None, None, :, None, None], right_flip[None, None, :, None, None])


def extend(values, margin, seams):
    batch_size, row_count, col_total, channels = values.shape
    local_strips = col_total // COL_DEV
    strips = values.reshape(batch_size, row_count, local_strips, COL_DEV, channels)
    rim_cols = jnp.concatenate(
        [strips[:, :, 0, :margin], strips[:, :, local_strips - 1, COL_DEV - margin :]], axis=2
    )
    padded = with_halo(rim_cols, (("strip", 2),), margin, True)
    halo_left = padded[:, :, :margin][:, :, None]
    halo_right = padded[:, :, 3 * margin :][:, :, None]
    from_left = jnp.concatenate(
        [halo_left, strips[:, :, : local_strips - 1, COL_DEV - margin :]], axis=2
    )
    from_right = jnp.concatenate([strips[:, :, 1:, :margin], halo_right], axis=2)
    from_left = jnp.where(seams[0], from_left[:, ::-1], from_left)
    from_right = jnp.where(seams[1], from_right[:, ::-1], from_right)
    widened = jnp.concatenate([from_left, strips, from_right], axis=3)
    rim_rows = jnp.concatenate([widened[:, :margin], widened[:, row_count - margin :]], axis=1)
    padded_rows = with_halo(rim_rows, (("blk", 1),), margin, False)
    return jnp.concatenate([padded_rows[:, :margin], widened, padded_rows[:, 3 * margin :]], axis=1)


def depthwise(widened, kernel, margin, row_count):
    batch_size, unused_rows, local_strips, unused_cols, channels = widened.shape
    summed = jnp.zeros((batch_size, row_count, local_strips, COL_DEV, channels), jnp.float32)
    for tap_row in range(3):
        for tap_col in range(3):
            tap_slice = widened[
                :,
                tap_row * margin : tap_row * margin + row_count,
                :,
                tap_col * margin : tap_col * margin + COL_DEV,
            ]
            summed = summed + tap_slice * kernel[3 * tap_row + tap_col]
    return summed.reshape(batch_size, row_count, local_strips * COL_DEV, channels)


def conv_back(widened, kernel, grad_pre, margin):
    batch_size, row_count, col_total, channels = grad_pre.shape
    unused, wide_rows, local_strips, wide_cols, unused_ch = widened.shape
    flat_wide = jnp.swapaxes(widened, 1, 2).reshape(-1, wide_rows, wide_cols, channels)
    grad_strips = grad_pre.reshape(batch_size, row_count, local_strips, COL_DEV, channels)
    flat_grad = jnp.swapaxes(grad_strips, 1, 2).reshape(-1, row_count, COL_DEV, channels)
    grad_wide, tap_sums = conv_back_kernel(flat_wide, flat_grad, kernel, margin)
    grad_wide = grad_wide.reshape(batch_size, local_strips, wide_rows, wide_cols, channels)
    return (tap_sums, jnp.swapaxes(grad_wide, 1, 2))


def fold_back(grad_wide, margin, seams):
    batch_size, wide_rows, local_strips, wide_cols, channels = grad_wide.shape
    row_count = wide_rows - 2 * margin
    rim_rows = jnp.concatenate([grad_wide[:, :margin], grad_wide[:, wide_rows - margin :]], axis=1)
    padded = with_halo(rim_rows.astype(jnp.bfloat16), (("blk", 1),), margin, False).astype(
        rim_rows.dtype
    )
    core_rows = grad_wide[:, margin : wide_rows - margin]
    no_pad = (0, 0)
    core_rows = core_rows + jnp.pad(
        padded[:, :margin], (no_pad, (0, row_count - margin), no_pad, no_pad, no_pad)
    )
    core_rows = core_rows + jnp.pad(
        padded[:, 3 * margin :], (no_pad, (row_count - margin, 0), no_pad, no_pad, no_pad)
    )
    left_part = core_rows[:, :, :, :margin]
    right_part = core_rows[:, :, :, wide_cols - margin :]
    left_part = jnp.where(seams[0], left_part[:, ::-1], left_part)
    right_part = jnp.where(seams[1], right_part[:, ::-1], right_part)
    rim_cols = jnp.concatenate([left_part[:, :, 0], right_part[:, :, local_strips - 1]], axis=2)
    padded_cols = with_halo(rim_cols.astype(jnp.bfloat16), (("strip", 2),), margin, True).astype(
        rim_cols.dtype
    )
    from_left_dev = padded_cols[:, :, :margin][:, :, None]
    from_right_dev = padded_cols[:, :, 3 * margin :][:, :, None]
    add_first = jnp.concatenate([from_left_dev, right_part[:, :, : local_strips - 1]], axis=2)
    add_last = jnp.concatenate([left_part[:, :, 1:], from_right_dev], axis=2)
    inner_cols = core_rows[:, :, :, margin : wide_cols - margin]
    inner_cols = inner_cols + jnp.pad(
        add_first, (no_pad, no_pad, no_pad, (0, COL_DEV - margin), no_pad)
    )
    inner_cols = inner_cols + jnp.pad(
        add_last, (no_pad, no_pad, no_pad, (COL_DEV - margin, 0), no_pad)
    )
    return inner_cols.reshape(batch_size, row_count, local_strips * COL_DEV, channels)


def pointwise(act, weight):
    channels = act.shape[-1]
    flat_act = act.reshape(-1, channels)
    return jnp.dot(flat_act, weight, preferred_element_type=jnp.float32).reshape(act.shape)


def block_back(widened, pre_val, act, grad_out, kernel, weight, margin, seams):
    channels = act.shape[-1]
    flat_grad = grad_out.reshape(-1, channels)
    d_weight = lax.dot_general(
        act.reshape(-1, channels),
        flat_grad,
        (((0,), (0,)), ((), ())),
        preferred_element_type=jnp.float32,
    )
    d_act = lax.dot_general(
        flat_grad, weight, (((1,), (1,)), ((), ())), preferred_element_type=jnp.float32
    ).reshape(pre_val.shape)
    logistic = jax.nn.sigmoid(pre_val)
    d_pre = d_act * logistic * (1.0 + pre_val * (1.0 - logistic))
    d_kernel, grad_wide = conv_back(widened, kernel, d_pre, margin)
    d_values = fold_back(grad_wide, margin, seams)
    grad_in = (grad_out.astype(jnp.float32) + d_values).astype(jnp.bfloat16)
    return (grad_in, d_kernel, d_weight)


def shards(fields, cotangent, kernel_one, weight_one, kernel_two, weight_two, seam_flags):
    batch_size, row_count, col_count, channels = fields.shape
    seams = seam_bits(seam_flags, col_count // COL_DEV)
    cells_all = (
        batch_size
        * row_count
        * col_count
        * lax.axis_size("strip")
        * lax.axis_size("blk")
        * lax.axis_size("dp")
    )
    factor = float(cells_all) ** (-0.5)
    wide_one = extend(fields, 1, seams).astype(jnp.float32)
    pre_one = depthwise(wide_one, kernel_one, 1, row_count)
    act_one = jax.nn.silu(pre_one).astype(jnp.bfloat16)
    hidden = (fields.astype(jnp.float32) + pointwise(act_one, weight_one)).astype(jnp.bfloat16)
    wide_two = extend(hidden, 2, seams).astype(jnp.float32)
    pre_two = depthwise(wide_two, kernel_two, 2, row_count)
    act_two = jax.nn.silu(pre_two).astype(jnp.bfloat16)
    grad_hidden, dk_two, dw_two = block_back(
        wide_two, pre_two, act_two, cotangent, kernel_two, weight_two, 2, seams
    )
    grad_fields, dk_one, dw_one = block_back(
        wide_one, pre_one, act_one, grad_hidden, kernel_one, weight_one, 1, seams
    )
    dk_one, dw_one, dk_two, dw_two = packed_sum(
        (dk_one, dw_one, dk_two, dw_two), ("strip", "blk", "dp"), tree_sum
    )
    return (grad_fields, dk_one * factor, dw_one * factor, dk_two * factor, dw_two * factor)


def solution(mesh):
    return jax.shard_map(
        shards,
        mesh=mesh,
        in_specs=(
            P("dp", "blk", "strip", None),
            P("dp", "blk", "strip", None),
            P(),
            P(),
            P(),
            P(),
            P(),
        ),
        out_specs=(P("dp", "blk", "strip", None), P(), P(), P(), P()),
        check_vma=False,
    )
```

```python
import jax
import jax.numpy as jnp
from jax import lax
from jax.sharding import PartitionSpec as P
from jax.experimental import pallas as pl
from jax.experimental.pallas import tpu as pltpu
import functools

COL_DEV = 16
ROW_BLOCK = 8


def tap_sum_body(margin, wide_ref, grad_ref, dk_ref):
    batch, wide_rows, wide_cols, channels = wide_ref.shape
    row_count = wide_rows - 2 * margin
    col_count = wide_cols - 2 * margin
    span = ROW_BLOCK + 2 * margin
    sums = [jnp.zeros((col_count, channels), jnp.float32) for _ in range(9)]
    for item in range(batch):

        def tap_step(step, sums):
            r0 = pl.multiple_of(step * ROW_BLOCK, ROW_BLOCK)
            grad = grad_ref[item, pl.ds(r0, ROW_BLOCK)]
            out = list(sums)
            for b in range(3):
                slab = wide_ref[item, pl.ds(r0, span), pl.ds(b * margin, col_count), :]
                for a in range(3):
                    seen = slab[a * margin : a * margin + ROW_BLOCK]
                    out[3 * a + b] = out[3 * a + b] + jnp.sum(seen * grad, axis=0)
            return out

        sums = lax.fori_loop(0, row_count // ROW_BLOCK, tap_step, sums)
    dk_ref[...] = jnp.concatenate([jnp.sum(s, axis=0, keepdims=True) for s in sums], axis=0)


def wide_grad_body(margin, grad_ref, k_ref, gw_ref, gpad_ref):
    batch, wide_rows, wide_cols, channels = gw_ref.shape
    row_count = wide_rows - 2 * margin
    col_count = wide_cols - 2 * margin
    kern = k_ref[...]
    for item in range(batch):
        gpad_ref[...] = jnp.zeros(gpad_ref.shape, jnp.float32)

        def fill_step(step, carry):
            r0 = pl.multiple_of(step * ROW_BLOCK, ROW_BLOCK)
            gpad_ref[pl.ds(r0 + 2 * margin, ROW_BLOCK), pl.ds(2 * margin, col_count), :] = grad_ref[
                item, pl.ds(r0, ROW_BLOCK)
            ]
            return carry

        lax.fori_loop(0, row_count // ROW_BLOCK, fill_step, 0)

        def wide_rows_at(r0, count):
            total = jnp.zeros((count, wide_cols, channels), jnp.float32)
            for b in range(3):
                slab = gpad_ref[pl.ds(r0, count + 2 * margin), pl.ds(2 * margin - b * margin, wide_cols), :]
                for a in range(3):
                    part = slab[2 * margin - a * margin : 2 * margin - a * margin + count]
                    total = total + part * kern[3 * a + b][None, None, :]
            gw_ref[item, pl.ds(r0, count), :, :] = total

        def wide_step(step, carry):
            wide_rows_at(pl.multiple_of(step * ROW_BLOCK, ROW_BLOCK), ROW_BLOCK)
            return carry

        full = wide_rows // ROW_BLOCK
        lax.fori_loop(0, full, wide_step, 0)
        if wide_rows - full * ROW_BLOCK:
            wide_rows_at(full * ROW_BLOCK, wide_rows - full * ROW_BLOCK)


def conv_back_kernel(wide, grad, kernel, margin):
    batch, wide_rows, wide_cols, channels = wide.shape
    elems = batch * wide_rows * wide_cols * channels
    pad_rows = grad.shape[1] + 4 * margin
    pad_cols = -(-(grad.shape[2] + 4 * margin) // 8) * 8
    vmem = pl.BlockSpec(memory_space=pltpu.VMEM)
    params = pltpu.CompilerParams(vmem_limit_bytes=48 * 1024 * 1024)
    grad_wide = pl.pallas_call(
        functools.partial(wide_grad_body, margin),
        out_shape=jax.ShapeDtypeStruct(wide.shape, jnp.float32),
        in_specs=[vmem, vmem],
        out_specs=vmem,
        scratch_shapes=[pltpu.VMEM((pad_rows, pad_cols, channels), jnp.float32)],
        compiler_params=params,
        cost_estimate=pl.CostEstimate(flops=18 * elems, bytes_accessed=8 * elems, transcendentals=0),
    )(grad, kernel)
    tap_sums = pl.pallas_call(
        functools.partial(tap_sum_body, margin),
        out_shape=jax.ShapeDtypeStruct((9, channels), jnp.float32),
        in_specs=[vmem, vmem],
        out_specs=vmem,
        compiler_params=params,
        cost_estimate=pl.CostEstimate(flops=18 * elems, bytes_accessed=8 * elems, transcendentals=0),
    )(wide.astype(jnp.float32), grad)
    return grad_wide, tap_sums


def tree_sum(value, axes):
    sizes = [lax.axis_size(axis) for axis in axes]
    count = 1
    for size in sizes:
        count *= size
    if count & (count - 1):
        return lax.psum(value, axes)
    bit = count // 2
    while bit >= 1:
        pairs = [(i, i ^ bit) for i in range(count)]
        value = value + lax.ppermute(value, axes, pairs)
        bit //= 2
    return value


def packed_sum(parts, axes, reducer):
    rows = [part.shape[0] for part in parts]
    summed = reducer(jnp.concatenate(parts, axis=0), axes)
    out, start = [], 0
    for count in rows:
        out.append(summed[start : start + count])
        start += count
    return out


def swap_halo(shard, axis, dim, width, length):
    last = lax.slice_in_dim(shard, length - width, length, axis=dim)
    first = lax.slice_in_dim(shard, 0, width, axis=dim)
    upper = lax.axis_index(axis) == 0
    sent = jnp.where(upper, last, first)
    got = lax.ppermute(sent, axis, [(0, 1), (1, 0)])
    zeros = jnp.zeros_like(got)
    before = jnp.where(upper, zeros, got)
    after = jnp.where(upper, got, zeros)
    return jnp.concatenate([before, shard, after], axis=dim)


def with_halo(shard, sides, width, wrap):
    for axis, dim in sides:
        count, length = (lax.axis_size(axis), shard.shape[dim])
        if count == 2 and not wrap:
            shard = swap_halo(shard, axis, dim, width, length)
            continue
        up = [(i, (i + 1) % count) for i in range(count if wrap else count - 1)]
        down = [(j, i) for i, j in up]
        last = lax.slice_in_dim(shard, length - width, length, axis=dim)
        first = lax.slice_in_dim(shard, 0, width, axis=dim)
        before = lax.ppermute(last, axis, up)
        after = lax.ppermute(first, axis, down)
        shard = jnp.concatenate([before, shard, after], axis=dim)
    return shard


def seam_bits(seam_flags, local_strips):
    circle_idx = lax.axis_index("blk")
    strip_idx = lax.axis_index("strip")
    strip_total = seam_flags.shape[1]
    circle_flags = lax.dynamic_index_in_dim(seam_flags, circle_idx, 0, keepdims=False)
    global_strip = strip_idx * local_strips + jnp.arange(local_strips, dtype=jnp.int32)
    next_strip = (global_strip + 1) % strip_total
    left_flip = jnp.take(circle_flags, global_strip) == 1
    right_flip = jnp.take(circle_flags, next_strip) == 1
    return (left_flip[None, None, :, None, None], right_flip[None, None, :, None, None])


def extend(values, margin, seams):
    batch_size, row_count, col_total, channels = values.shape
    local_strips = col_total // COL_DEV
    strips = values.reshape(batch_size, row_count, local_strips, COL_DEV, channels)
    rim_cols = jnp.concatenate(
        [strips[:, :, 0, :margin], strips[:, :, local_strips - 1, COL_DEV - margin :]], axis=2
    )
    padded = with_halo(rim_cols, (("strip", 2),), margin, True)
    halo_left = padded[:, :, :margin][:, :, None]
    halo_right = padded[:, :, 3 * margin :][:, :, None]
    from_left = jnp.concatenate(
        [halo_left, strips[:, :, : local_strips - 1, COL_DEV - margin :]], axis=2
    )
    from_right = jnp.concatenate([strips[:, :, 1:, :margin], halo_right], axis=2)
    from_left = jnp.where(seams[0], from_left[:, ::-1], from_left)
    from_right = jnp.where(seams[1], from_right[:, ::-1], from_right)
    widened = jnp.concatenate([from_left, strips, from_right], axis=3)
    rim_rows = jnp.concatenate([widened[:, :margin], widened[:, row_count - margin :]], axis=1)
    padded_rows = with_halo(rim_rows, (("blk", 1),), margin, False)
    return jnp.concatenate([padded_rows[:, :margin], widened, padded_rows[:, 3 * margin :]], axis=1)


def depthwise(widened, kernel, margin, row_count):
    batch_size, unused_rows, local_strips, unused_cols, channels = widened.shape
    summed = jnp.zeros((batch_size, row_count, local_strips, COL_DEV, channels), jnp.float32)
    for tap_row in range(3):
        for tap_col in range(3):
            tap_slice = widened[
                :,
                tap_row * margin : tap_row * margin + row_count,
                :,
                tap_col * margin : tap_col * margin + COL_DEV,
            ]
            summed = summed + tap_slice * kernel[3 * tap_row + tap_col]
    return summed.reshape(batch_size, row_count, local_strips * COL_DEV, channels)


def conv_back(widened, kernel, grad_pre, margin):
    batch_size, row_count, col_total, channels = grad_pre.shape
    unused, wide_rows, local_strips, wide_cols, unused_ch = widened.shape
    flat_wide = jnp.swapaxes(widened, 1, 2).reshape(-1, wide_rows, wide_cols, channels)
    grad_strips = grad_pre.reshape(batch_size, row_count, local_strips, COL_DEV, channels)
    flat_grad = jnp.swapaxes(grad_strips, 1, 2).reshape(-1, row_count, COL_DEV, channels)
    grad_wide, tap_sums = conv_back_kernel(flat_wide, flat_grad, kernel, margin)
    grad_wide = grad_wide.reshape(batch_size, local_strips, wide_rows, wide_cols, channels)
    return (tap_sums, jnp.swapaxes(grad_wide, 1, 2))


def fold_back(grad_wide, margin, seams):
    batch_size, wide_rows, local_strips, wide_cols, channels = grad_wide.shape
    row_count = wide_rows - 2 * margin
    rim_rows = jnp.concatenate([grad_wide[:, :margin], grad_wide[:, wide_rows - margin :]], axis=1)
    padded = with_halo(rim_rows.astype(jnp.bfloat16), (("blk", 1),), margin, False).astype(
        rim_rows.dtype
    )
    core_rows = grad_wide[:, margin : wide_rows - margin]
    no_pad = (0, 0)
    core_rows = core_rows + jnp.pad(
        padded[:, :margin], (no_pad, (0, row_count - margin), no_pad, no_pad, no_pad)
    )
    core_rows = core_rows + jnp.pad(
        padded[:, 3 * margin :], (no_pad, (row_count - margin, 0), no_pad, no_pad, no_pad)
    )
    left_part = core_rows[:, :, :, :margin]
    right_part = core_rows[:, :, :, wide_cols - margin :]
    left_part = jnp.where(seams[0], left_part[:, ::-1], left_part)
    right_part = jnp.where(seams[1], right_part[:, ::-1], right_part)
    rim_cols = jnp.concatenate([left_part[:, :, 0], right_part[:, :, local_strips - 1]], axis=2)
    padded_cols = with_halo(rim_cols.astype(jnp.bfloat16), (("strip", 2),), margin, True).astype(
        rim_cols.dtype
    )
    from_left_dev = padded_cols[:, :, :margin][:, :, None]
    from_right_dev = padded_cols[:, :, 3 * margin :][:, :, None]
    add_first = jnp.concatenate([from_left_dev, right_part[:, :, : local_strips - 1]], axis=2)
    add_last = jnp.concatenate([left_part[:, :, 1:], from_right_dev], axis=2)
    inner_cols = core_rows[:, :, :, margin : wide_cols - margin]
    inner_cols = inner_cols + jnp.pad(
        add_first, (no_pad, no_pad, no_pad, (0, COL_DEV - margin), no_pad)
    )
    inner_cols = inner_cols + jnp.pad(
        add_last, (no_pad, no_pad, no_pad, (COL_DEV - margin, 0), no_pad)
    )
    return inner_cols.reshape(batch_size, row_count, local_strips * COL_DEV, channels)


def pointwise(act, weight):
    channels = act.shape[-1]
    flat_act = act.reshape(-1, channels)
    return jnp.dot(flat_act, weight, preferred_element_type=jnp.float32).reshape(act.shape)


def block_back(widened, pre_val, act, grad_out, kernel, weight, margin, seams):
    channels = act.shape[-1]
    flat_grad = grad_out.reshape(-1, channels)
    d_weight = lax.dot_general(
        act.reshape(-1, channels),
        flat_grad,
        (((0,), (0,)), ((), ())),
        preferred_element_type=jnp.float32,
    )
    d_act = lax.dot_general(
        flat_grad, weight, (((1,), (1,)), ((), ())), preferred_element_type=jnp.float32
    ).reshape(pre_val.shape)
    logistic = jax.nn.sigmoid(pre_val)
    d_pre = d_act * logistic * (1.0 + pre_val * (1.0 - logistic))
    d_kernel, grad_wide = conv_back(widened, kernel, d_pre, margin)
    d_values = fold_back(grad_wide, margin, seams)
    grad_in = (grad_out.astype(jnp.float32) + d_values).astype(jnp.bfloat16)
    return (grad_in, d_kernel, d_weight)


def shards(fields, cotangent, kernel_one, weight_one, kernel_two, weight_two, seam_flags):
    batch_size, row_count, col_count, channels = fields.shape
    seams = seam_bits(seam_flags, col_count // COL_DEV)
    cells_all = (
        batch_size
        * row_count
        * col_count
        * lax.axis_size("strip")
        * lax.axis_size("blk")
        * lax.axis_size("dp")
    )
    factor = float(cells_all) ** (-0.5)
    wide_one = extend(fields, 1, seams).astype(jnp.float32)
    pre_one = depthwise(wide_one, kernel_one, 1, row_count)
    act_one = jax.nn.silu(pre_one).astype(jnp.bfloat16)
    hidden = (fields.astype(jnp.float32) + pointwise(act_one, weight_one)).astype(jnp.bfloat16)
    wide_two = extend(hidden, 2, seams).astype(jnp.float32)
    pre_two = depthwise(wide_two, kernel_two, 2, row_count)
    act_two = jax.nn.silu(pre_two).astype(jnp.bfloat16)
    grad_hidden, dk_two, dw_two = block_back(
        wide_two, pre_two, act_two, cotangent, kernel_two, weight_two, 2, seams
    )
    grad_fields, dk_one, dw_one = block_back(
        wide_one, pre_one, act_one, grad_hidden, kernel_one, weight_one, 1, seams
    )
    dk_one, dw_one, dk_two, dw_two = packed_sum(
        (dk_one, dw_one, dk_two, dw_two), ("strip", "blk", "dp"), tree_sum
    )
    return (grad_fields, dk_one * factor, dw_one * factor, dk_two * factor, dw_two * factor)


def solution(mesh):
    return jax.shard_map(
        shards,
        mesh=mesh,
        in_specs=(
            P("dp", "blk", "strip", None),
            P("dp", "blk", "strip", None),
            P(),
            P(),
            P(),
            P(),
            P(),
        ),
        out_specs=(P("dp", "blk", "strip", None), P(), P(), P(), P()),
        check_vma=False,
    )
```

```python
import jax
import jax.numpy as jnp
from jax import lax
from jax.sharding import PartitionSpec as P
from jax.experimental import pallas as pl
from jax.experimental.pallas import tpu as pltpu
import functools

COL_DEV = 16
ROW_BLOCK = 8


def tap_sum_body(margin, wide_ref, grad_ref, dk_ref):
    batch, wide_rows, wide_cols, channels = wide_ref.shape
    row_count = wide_rows - 2 * margin
    col_count = wide_cols - 2 * margin
    span = ROW_BLOCK + 2 * margin
    sums = [jnp.zeros((col_count, channels), jnp.float32) for _ in range(9)]
    for item in range(batch):

        def tap_step(step, sums):
            r0 = pl.multiple_of(step * ROW_BLOCK, ROW_BLOCK)
            grad = grad_ref[item, pl.ds(r0, ROW_BLOCK)]
            out = list(sums)
            for b in range(3):
                slab = wide_ref[item, pl.ds(r0, span), pl.ds(b * margin, col_count), :]
                for a in range(3):
                    seen = slab[a * margin : a * margin + ROW_BLOCK]
                    out[3 * a + b] = out[3 * a + b] + jnp.sum(seen * grad, axis=0)
            return out

        sums = lax.fori_loop(0, row_count // ROW_BLOCK, tap_step, sums)
    dk_ref[...] = jnp.concatenate([jnp.sum(s, axis=0, keepdims=True) for s in sums], axis=0)


def wide_grad_body(margin, grad_ref, k_ref, gw_ref, gpad_ref):
    batch, wide_rows, wide_cols, channels = gw_ref.shape
    row_count = wide_rows - 2 * margin
    col_count = wide_cols - 2 * margin
    kern = k_ref[...]
    for item in range(batch):
        gpad_ref[...] = jnp.zeros(gpad_ref.shape, jnp.float32)

        def fill_step(step, carry):
            r0 = pl.multiple_of(step * ROW_BLOCK, ROW_BLOCK)
            gpad_ref[pl.ds(r0 + 2 * margin, ROW_BLOCK), pl.ds(2 * margin, col_count), :] = grad_ref[
                item, pl.ds(r0, ROW_BLOCK)
            ]
            return carry

        lax.fori_loop(0, row_count // ROW_BLOCK, fill_step, 0)

        def wide_rows_at(r0, count):
            total = jnp.zeros((count, wide_cols, channels), jnp.float32)
            for b in range(3):
                slab = gpad_ref[pl.ds(r0, count + 2 * margin), pl.ds(2 * margin - b * margin, wide_cols), :]
                for a in range(3):
                    part = slab[2 * margin - a * margin : 2 * margin - a * margin + count]
                    total = total + part * kern[3 * a + b][None, None, :]
            gw_ref[item, pl.ds(r0, count), :, :] = total

        def wide_step(step, carry):
            wide_rows_at(pl.multiple_of(step * ROW_BLOCK, ROW_BLOCK), ROW_BLOCK)
            return carry

        full = wide_rows // ROW_BLOCK
        lax.fori_loop(0, full, wide_step, 0)
        if wide_rows - full * ROW_BLOCK:
            wide_rows_at(full * ROW_BLOCK, wide_rows - full * ROW_BLOCK)


def conv_back_kernel(wide, grad, kernel, margin):
    batch, wide_rows, wide_cols, channels = wide.shape
    elems = batch * wide_rows * wide_cols * channels
    pad_rows = grad.shape[1] + 4 * margin
    pad_cols = -(-(grad.shape[2] + 4 * margin) // 8) * 8
    vmem = pl.BlockSpec(memory_space=pltpu.VMEM)
    params = pltpu.CompilerParams(vmem_limit_bytes=16 * 1024 * 1024)
    grad_wide = pl.pallas_call(
        functools.partial(wide_grad_body, margin),
        out_shape=jax.ShapeDtypeStruct(wide.shape, jnp.float32),
        in_specs=[vmem, vmem],
        out_specs=vmem,
        scratch_shapes=[pltpu.VMEM((pad_rows, pad_cols, channels), jnp.float32)],
        compiler_params=params,
        cost_estimate=pl.CostEstimate(flops=18 * elems, bytes_accessed=8 * elems, transcendentals=0),
    )(grad, kernel)
    tap_sums = pl.pallas_call(
        functools.partial(tap_sum_body, margin),
        out_shape=jax.ShapeDtypeStruct((9, channels), jnp.float32),
        in_specs=[vmem, vmem],
        out_specs=vmem,
        compiler_params=params,
        cost_estimate=pl.CostEstimate(flops=18 * elems, bytes_accessed=8 * elems, transcendentals=0),
    )(wide.astype(jnp.float32), grad)
    return grad_wide, tap_sums


def tree_sum(value, axes):
    sizes = [lax.axis_size(axis) for axis in axes]
    count = 1
    for size in sizes:
        count *= size
    if count & (count - 1):
        return lax.psum(value, axes)
    bit = count // 2
    while bit >= 1:
        pairs = [(i, i ^ bit) for i in range(count)]
        value = value + lax.ppermute(value, axes, pairs)
        bit //= 2
    return value


def packed_sum(parts, axes, reducer):
    rows = [part.shape[0] for part in parts]
    summed = reducer(jnp.concatenate(parts, axis=0), axes)
    out, start = [], 0
    for count in rows:
        out.append(summed[start : start + count])
        start += count
    return out


def swap_halo(shard, axis, dim, width, length):
    last = lax.slice_in_dim(shard, length - width, length, axis=dim)
    first = lax.slice_in_dim(shard, 0, width, axis=dim)
    upper = lax.axis_index(axis) == 0
    sent = jnp.where(upper, last, first)
    got = lax.ppermute(sent, axis, [(0, 1), (1, 0)])
    zeros = jnp.zeros_like(got)
    before = jnp.where(upper, zeros, got)
    after = jnp.where(upper, got, zeros)
    return jnp.concatenate([before, shard, after], axis=dim)


def with_halo(shard, sides, width, wrap):
    for axis, dim in sides:
        count, length = (lax.axis_size(axis), shard.shape[dim])
        if count == 2 and not wrap:
            shard = swap_halo(shard, axis, dim, width, length)
            continue
        up = [(i, (i + 1) % count) for i in range(count if wrap else count - 1)]
        down = [(j, i) for i, j in up]
        last = lax.slice_in_dim(shard, length - width, length, axis=dim)
        first = lax.slice_in_dim(shard, 0, width, axis=dim)
        before = lax.ppermute(last, axis, up)
        after = lax.ppermute(first, axis, down)
        shard = jnp.concatenate([before, shard, after], axis=dim)
    return shard


def seam_bits(seam_flags, local_strips):
    circle_idx = lax.axis_index("blk")
    strip_idx = lax.axis_index("strip")
    strip_total = seam_flags.shape[1]
    circle_flags = lax.dynamic_index_in_dim(seam_flags, circle_idx, 0, keepdims=False)
    global_strip = strip_idx * local_strips + jnp.arange(local_strips, dtype=jnp.int32)
    next_strip = (global_strip + 1) % strip_total
    left_flip = jnp.take(circle_flags, global_strip) == 1
    right_flip = jnp.take(circle_flags, next_strip) == 1
    return (left_flip[None, None, :, None, None], right_flip[None, None, :, None, None])


def extend(values, margin, seams):
    batch_size, row_count, col_total, channels = values.shape
    local_strips = col_total // COL_DEV
    strips = values.reshape(batch_size, row_count, local_strips, COL_DEV, channels)
    rim_cols = jnp.concatenate(
        [strips[:, :, 0, :margin], strips[:, :, local_strips - 1, COL_DEV - margin :]], axis=2
    )
    padded = with_halo(rim_cols, (("strip", 2),), margin, True)
    halo_left = padded[:, :, :margin][:, :, None]
    halo_right = padded[:, :, 3 * margin :][:, :, None]
    from_left = jnp.concatenate(
        [halo_left, strips[:, :, : local_strips - 1, COL_DEV - margin :]], axis=2
    )
    from_right = jnp.concatenate([strips[:, :, 1:, :margin], halo_right], axis=2)
    from_left = jnp.where(seams[0], from_left[:, ::-1], from_left)
    from_right = jnp.where(seams[1], from_right[:, ::-1], from_right)
    widened = jnp.concatenate([from_left, strips, from_right], axis=3)
    rim_rows = jnp.concatenate([widened[:, :margin], widened[:, row_count - margin :]], axis=1)
    padded_rows = with_halo(rim_rows, (("blk", 1),), margin, False)
    return jnp.concatenate([padded_rows[:, :margin], widened, padded_rows[:, 3 * margin :]], axis=1)


def depthwise(widened, kernel, margin, row_count):
    batch_size, unused_rows, local_strips, unused_cols, channels = widened.shape
    summed = jnp.zeros((batch_size, row_count, local_strips, COL_DEV, channels), jnp.float32)
    for tap_row in range(3):
        for tap_col in range(3):
            tap_slice = widened[
                :,
                tap_row * margin : tap_row * margin + row_count,
                :,
                tap_col * margin : tap_col * margin + COL_DEV,
            ]
            summed = summed + tap_slice * kernel[3 * tap_row + tap_col]
    return summed.reshape(batch_size, row_count, local_strips * COL_DEV, channels)


def conv_back(widened, kernel, grad_pre, margin):
    batch_size, row_count, col_total, channels = grad_pre.shape
    unused, wide_rows, local_strips, wide_cols, unused_ch = widened.shape
    flat_wide = jnp.swapaxes(widened, 1, 2).reshape(-1, wide_rows, wide_cols, channels)
    grad_strips = grad_pre.reshape(batch_size, row_count, local_strips, COL_DEV, channels)
    flat_grad = jnp.swapaxes(grad_strips, 1, 2).reshape(-1, row_count, COL_DEV, channels)
    grad_wide, tap_sums = conv_back_kernel(flat_wide, flat_grad, kernel, margin)
    grad_wide = grad_wide.reshape(batch_size, local_strips, wide_rows, wide_cols, channels)
    return (tap_sums, jnp.swapaxes(grad_wide, 1, 2))


def fold_back(grad_wide, margin, seams):
    batch_size, wide_rows, local_strips, wide_cols, channels = grad_wide.shape
    row_count = wide_rows - 2 * margin
    rim_rows = jnp.concatenate([grad_wide[:, :margin], grad_wide[:, wide_rows - margin :]], axis=1)
    padded = with_halo(rim_rows.astype(jnp.bfloat16), (("blk", 1),), margin, False).astype(
        rim_rows.dtype
    )
    core_rows = grad_wide[:, margin : wide_rows - margin]
    no_pad = (0, 0)
    core_rows = core_rows + jnp.pad(
        padded[:, :margin], (no_pad, (0, row_count - margin), no_pad, no_pad, no_pad)
    )
    core_rows = core_rows + jnp.pad(
        padded[:, 3 * margin :], (no_pad, (row_count - margin, 0), no_pad, no_pad, no_pad)
    )
    left_part = core_rows[:, :, :, :margin]
    right_part = core_rows[:, :, :, wide_cols - margin :]
    left_part = jnp.where(seams[0], left_part[:, ::-1], left_part)
    right_part = jnp.where(seams[1], right_part[:, ::-1], right_part)
    rim_cols = jnp.concatenate([left_part[:, :, 0], right_part[:, :, local_strips - 1]], axis=2)
    padded_cols = with_halo(rim_cols.astype(jnp.bfloat16), (("strip", 2),), margin, True).astype(
        rim_cols.dtype
    )
    from_left_dev = padded_cols[:, :, :margin][:, :, None]
    from_right_dev = padded_cols[:, :, 3 * margin :][:, :, None]
    add_first = jnp.concatenate([from_left_dev, right_part[:, :, : local_strips - 1]], axis=2)
    add_last = jnp.concatenate([left_part[:, :, 1:], from_right_dev], axis=2)
    inner_cols = core_rows[:, :, :, margin : wide_cols - margin]
    inner_cols = inner_cols + jnp.pad(
        add_first, (no_pad, no_pad, no_pad, (0, COL_DEV - margin), no_pad)
    )
    inner_cols = inner_cols + jnp.pad(
        add_last, (no_pad, no_pad, no_pad, (COL_DEV - margin, 0), no_pad)
    )
    return inner_cols.reshape(batch_size, row_count, local_strips * COL_DEV, channels)


def pointwise(act, weight):
    channels = act.shape[-1]
    flat_act = act.reshape(-1, channels)
    return jnp.dot(flat_act, weight, preferred_element_type=jnp.float32).reshape(act.shape)


def block_back(widened, pre_val, act, grad_out, kernel, weight, margin, seams):
    channels = act.shape[-1]
    flat_grad = grad_out.reshape(-1, channels)
    d_weight = lax.dot_general(
        act.reshape(-1, channels),
        flat_grad,
        (((0,), (0,)), ((), ())),
        preferred_element_type=jnp.float32,
    )
    d_act = lax.dot_general(
        flat_grad, weight, (((1,), (1,)), ((), ())), preferred_element_type=jnp.float32
    ).reshape(pre_val.shape)
    logistic = jax.nn.sigmoid(pre_val)
    d_pre = d_act * logistic * (1.0 + pre_val * (1.0 - logistic))
    d_kernel, grad_wide = conv_back(widened, kernel, d_pre, margin)
    d_values = fold_back(grad_wide, margin, seams)
    grad_in = (grad_out.astype(jnp.float32) + d_values).astype(jnp.bfloat16)
    return (grad_in, d_kernel, d_weight)


def shards(fields, cotangent, kernel_one, weight_one, kernel_two, weight_two, seam_flags):
    batch_size, row_count, col_count, channels = fields.shape
    seams = seam_bits(seam_flags, col_count // COL_DEV)
    cells_all = (
        batch_size
        * row_count
        * col_count
        * lax.axis_size("strip")
        * lax.axis_size("blk")
        * lax.axis_size("dp")
    )
    factor = float(cells_all) ** (-0.5)
    wide_one = extend(fields, 1, seams).astype(jnp.float32)
    pre_one = depthwise(wide_one, kernel_one, 1, row_count)
    act_one = jax.nn.silu(pre_one).astype(jnp.bfloat16)
    hidden = (fields.astype(jnp.float32) + pointwise(act_one, weight_one)).astype(jnp.bfloat16)
    wide_two = extend(hidden, 2, seams).astype(jnp.float32)
    pre_two = depthwise(wide_two, kernel_two, 2, row_count)
    act_two = jax.nn.silu(pre_two).astype(jnp.bfloat16)
    grad_hidden, dk_two, dw_two = block_back(
        wide_two, pre_two, act_two, cotangent, kernel_two, weight_two, 2, seams
    )
    grad_fields, dk_one, dw_one = block_back(
        wide_one, pre_one, act_one, grad_hidden, kernel_one, weight_one, 1, seams
    )
    dk_one, dw_one, dk_two, dw_two = packed_sum(
        (dk_one, dw_one, dk_two, dw_two), ("strip", "blk", "dp"), tree_sum
    )
    return (grad_fields, dk_one * factor, dw_one * factor, dk_two * factor, dw_two * factor)


def solution(mesh):
    return jax.shard_map(
        shards,
        mesh=mesh,
        in_specs=(
            P("dp", "blk", "strip", None),
            P("dp", "blk", "strip", None),
            P(),
            P(),
            P(),
            P(),
            P(),
        ),
        out_specs=(P("dp", "blk", "strip", None), P(), P(), P(), P()),
        check_vma=False,
    )
```

```python
import jax
import jax.numpy as jnp
from jax import lax
from jax.sharding import PartitionSpec as P
from jax.experimental import pallas as pl
from jax.experimental.pallas import tpu as pltpu
import functools

COL_DEV = 16
ROW_BLOCK = 16


def tap_sum_body(margin, wide_ref, grad_ref, dk_ref):
    batch, wide_rows, wide_cols, channels = wide_ref.shape
    row_count = wide_rows - 2 * margin
    col_count = wide_cols - 2 * margin
    span = ROW_BLOCK + 2 * margin
    sums = [jnp.zeros((col_count, channels), jnp.float32) for _ in range(9)]
    for item in range(batch):

        def tap_step(step, sums):
            r0 = pl.multiple_of(step * ROW_BLOCK, ROW_BLOCK)
            grad = grad_ref[item, pl.ds(r0, ROW_BLOCK)]
            out = list(sums)
            for b in range(3):
                slab = wide_ref[item, pl.ds(r0, span), pl.ds(b * margin, col_count), :]
                for a in range(3):
                    seen = slab[a * margin : a * margin + ROW_BLOCK]
                    out[3 * a + b] = out[3 * a + b] + jnp.sum(seen * grad, axis=0)
            return out

        sums = lax.fori_loop(0, row_count // ROW_BLOCK, tap_step, sums)
    dk_ref[...] = jnp.concatenate([jnp.sum(s, axis=0, keepdims=True) for s in sums], axis=0)


def wide_grad_body(margin, grad_ref, k_ref, gw_ref, gpad_ref):
    batch, wide_rows, wide_cols, channels = gw_ref.shape
    row_count = wide_rows - 2 * margin
    col_count = wide_cols - 2 * margin
    kern = k_ref[...]
    for item in range(batch):
        gpad_ref[...] = jnp.zeros(gpad_ref.shape, jnp.float32)

        def fill_step(step, carry):
            r0 = pl.multiple_of(step * ROW_BLOCK, ROW_BLOCK)
            gpad_ref[pl.ds(r0 + 2 * margin, ROW_BLOCK), pl.ds(2 * margin, col_count), :] = grad_ref[
                item, pl.ds(r0, ROW_BLOCK)
            ]
            return carry

        lax.fori_loop(0, row_count // ROW_BLOCK, fill_step, 0)

        def wide_rows_at(r0, count):
            total = jnp.zeros((count, wide_cols, channels), jnp.float32)
            for b in range(3):
                slab = gpad_ref[pl.ds(r0, count + 2 * margin), pl.ds(2 * margin - b * margin, wide_cols), :]
                for a in range(3):
                    part = slab[2 * margin - a * margin : 2 * margin - a * margin + count]
                    total = total + part * kern[3 * a + b][None, None, :]
            gw_ref[item, pl.ds(r0, count), :, :] = total

        def wide_step(step, carry):
            wide_rows_at(pl.multiple_of(step * ROW_BLOCK, ROW_BLOCK), ROW_BLOCK)
            return carry

        full = wide_rows // ROW_BLOCK
        lax.fori_loop(0, full, wide_step, 0)
        if wide_rows - full * ROW_BLOCK:
            wide_rows_at(full * ROW_BLOCK, wide_rows - full * ROW_BLOCK)


def conv_back_kernel(wide, grad, kernel, margin):
    batch, wide_rows, wide_cols, channels = wide.shape
    elems = batch * wide_rows * wide_cols * channels
    pad_rows = grad.shape[1] + 4 * margin
    pad_cols = -(-(grad.shape[2] + 4 * margin) // 8) * 8
    vmem = pl.BlockSpec(memory_space=pltpu.VMEM)
    params = pltpu.CompilerParams(vmem_limit_bytes=4 * 1024 * 1024)
    grad_wide = pl.pallas_call(
        functools.partial(wide_grad_body, margin),
        out_shape=jax.ShapeDtypeStruct(wide.shape, jnp.float32),
        in_specs=[vmem, vmem],
        out_specs=vmem,
        scratch_shapes=[pltpu.VMEM((pad_rows, pad_cols, channels), jnp.float32)],
        compiler_params=params,
        cost_estimate=pl.CostEstimate(flops=18 * elems, bytes_accessed=8 * elems, transcendentals=0),
    )(grad, kernel)
    tap_sums = pl.pallas_call(
        functools.partial(tap_sum_body, margin),
        out_shape=jax.ShapeDtypeStruct((9, channels), jnp.float32),
        in_specs=[vmem, vmem],
        out_specs=vmem,
        compiler_params=params,
        cost_estimate=pl.CostEstimate(flops=18 * elems, bytes_accessed=8 * elems, transcendentals=0),
    )(wide.astype(jnp.float32), grad)
    return grad_wide, tap_sums


def tree_sum(value, axes):
    sizes = [lax.axis_size(axis) for axis in axes]
    count = 1
    for size in sizes:
        count *= size
    if count & (count - 1):
        return lax.psum(value, axes)
    bit = count // 2
    while bit >= 1:
        pairs = [(i, i ^ bit) for i in range(count)]
        value = value + lax.ppermute(value, axes, pairs)
        bit //= 2
    return value


def packed_sum(parts, axes, reducer):
    rows = [part.shape[0] for part in parts]
    summed = reducer(jnp.concatenate(parts, axis=0), axes)
    out, start = [], 0
    for count in rows:
        out.append(summed[start : start + count])
        start += count
    return out


def swap_halo(shard, axis, dim, width, length):
    last = lax.slice_in_dim(shard, length - width, length, axis=dim)
    first = lax.slice_in_dim(shard, 0, width, axis=dim)
    upper = lax.axis_index(axis) == 0
    sent = jnp.where(upper, last, first)
    got = lax.ppermute(sent, axis, [(0, 1), (1, 0)])
    zeros = jnp.zeros_like(got)
    before = jnp.where(upper, zeros, got)
    after = jnp.where(upper, got, zeros)
    return jnp.concatenate([before, shard, after], axis=dim)


def with_halo(shard, sides, width, wrap):
    for axis, dim in sides:
        count, length = (lax.axis_size(axis), shard.shape[dim])
        if count == 2 and not wrap:
            shard = swap_halo(shard, axis, dim, width, length)
            continue
        up = [(i, (i + 1) % count) for i in range(count if wrap else count - 1)]
        down = [(j, i) for i, j in up]
        last = lax.slice_in_dim(shard, length - width, length, axis=dim)
        first = lax.slice_in_dim(shard, 0, width, axis=dim)
        before = lax.ppermute(last, axis, up)
        after = lax.ppermute(first, axis, down)
        shard = jnp.concatenate([before, shard, after], axis=dim)
    return shard


def seam_bits(seam_flags, local_strips):
    circle_idx = lax.axis_index("blk")
    strip_idx = lax.axis_index("strip")
    strip_total = seam_flags.shape[1]
    circle_flags = lax.dynamic_index_in_dim(seam_flags, circle_idx, 0, keepdims=False)
    global_strip = strip_idx * local_strips + jnp.arange(local_strips, dtype=jnp.int32)
    next_strip = (global_strip + 1) % strip_total
    left_flip = jnp.take(circle_flags, global_strip) == 1
    right_flip = jnp.take(circle_flags, next_strip) == 1
    return (left_flip[None, None, :, None, None], right_flip[None, None, :, None, None])


def extend(values, margin, seams):
    batch_size, row_count, col_total, channels = values.shape
    local_strips = col_total // COL_DEV
    strips = values.reshape(batch_size, row_count, local_strips, COL_DEV, channels)
    rim_cols = jnp.concatenate(
        [strips[:, :, 0, :margin], strips[:, :, local_strips - 1, COL_DEV - margin :]], axis=2
    )
    padded = with_halo(rim_cols, (("strip", 2),), margin, True)
    halo_left = padded[:, :, :margin][:, :, None]
    halo_right = padded[:, :, 3 * margin :][:, :, None]
    from_left = jnp.concatenate(
        [halo_left, strips[:, :, : local_strips - 1, COL_DEV - margin :]], axis=2
    )
    from_right = jnp.concatenate([strips[:, :, 1:, :margin], halo_right], axis=2)
    from_left = jnp.where(seams[0], from_left[:, ::-1], from_left)
    from_right = jnp.where(seams[1], from_right[:, ::-1], from_right)
    widened = jnp.concatenate([from_left, strips, from_right], axis=3)
    rim_rows = jnp.concatenate([widened[:, :margin], widened[:, row_count - margin :]], axis=1)
    padded_rows = with_halo(rim_rows, (("blk", 1),), margin, False)
    return jnp.concatenate([padded_rows[:, :margin], widened, padded_rows[:, 3 * margin :]], axis=1)


def depthwise(widened, kernel, margin, row_count):
    batch_size, unused_rows, local_strips, unused_cols, channels = widened.shape
    summed = jnp.zeros((batch_size, row_count, local_strips, COL_DEV, channels), jnp.float32)
    for tap_row in range(3):
        for tap_col in range(3):
            tap_slice = widened[
                :,
                tap_row * margin : tap_row * margin + row_count,
                :,
                tap_col * margin : tap_col * margin + COL_DEV,
            ]
            summed = summed + tap_slice * kernel[3 * tap_row + tap_col]
    return summed.reshape(batch_size, row_count, local_strips * COL_DEV, channels)


def conv_back(widened, kernel, grad_pre, margin):
    batch_size, row_count, col_total, channels = grad_pre.shape
    unused, wide_rows, local_strips, wide_cols, unused_ch = widened.shape
    flat_wide = jnp.swapaxes(widened, 1, 2).reshape(-1, wide_rows, wide_cols, channels)
    grad_strips = grad_pre.reshape(batch_size, row_count, local_strips, COL_DEV, channels)
    flat_grad = jnp.swapaxes(grad_strips, 1, 2).reshape(-1, row_count, COL_DEV, channels)
    grad_wide, tap_sums = conv_back_kernel(flat_wide, flat_grad, kernel, margin)
    grad_wide = grad_wide.reshape(batch_size, local_strips, wide_rows, wide_cols, channels)
    return (tap_sums, jnp.swapaxes(grad_wide, 1, 2))


def fold_back(grad_wide, margin, seams):
    batch_size, wide_rows, local_strips, wide_cols, channels = grad_wide.shape
    row_count = wide_rows - 2 * margin
    rim_rows = jnp.concatenate([grad_wide[:, :margin], grad_wide[:, wide_rows - margin :]], axis=1)
    padded = with_halo(rim_rows.astype(jnp.bfloat16), (("blk", 1),), margin, False).astype(
        rim_rows.dtype
    )
    core_rows = grad_wide[:, margin : wide_rows - margin]
    no_pad = (0, 0)
    core_rows = core_rows + jnp.pad(
        padded[:, :margin], (no_pad, (0, row_count - margin), no_pad, no_pad, no_pad)
    )
    core_rows = core_rows + jnp.pad(
        padded[:, 3 * margin :], (no_pad, (row_count - margin, 0), no_pad, no_pad, no_pad)
    )
    left_part = core_rows[:, :, :, :margin]
    right_part = core_rows[:, :, :, wide_cols - margin :]
    left_part = jnp.where(seams[0], left_part[:, ::-1], left_part)
    right_part = jnp.where(seams[1], right_part[:, ::-1], right_part)
    rim_cols = jnp.concatenate([left_part[:, :, 0], right_part[:, :, local_strips - 1]], axis=2)
    padded_cols = with_halo(rim_cols.astype(jnp.bfloat16), (("strip", 2),), margin, True).astype(
        rim_cols.dtype
    )
    from_left_dev = padded_cols[:, :, :margin][:, :, None]
    from_right_dev = padded_cols[:, :, 3 * margin :][:, :, None]
    add_first = jnp.concatenate([from_left_dev, right_part[:, :, : local_strips - 1]], axis=2)
    add_last = jnp.concatenate([left_part[:, :, 1:], from_right_dev], axis=2)
    inner_cols = core_rows[:, :, :, margin : wide_cols - margin]
    inner_cols = inner_cols + jnp.pad(
        add_first, (no_pad, no_pad, no_pad, (0, COL_DEV - margin), no_pad)
    )
    inner_cols = inner_cols + jnp.pad(
        add_last, (no_pad, no_pad, no_pad, (COL_DEV - margin, 0), no_pad)
    )
    return inner_cols.reshape(batch_size, row_count, local_strips * COL_DEV, channels)


def pointwise(act, weight):
    channels = act.shape[-1]
    flat_act = act.reshape(-1, channels)
    return jnp.dot(flat_act, weight, preferred_element_type=jnp.float32).reshape(act.shape)


def block_back(widened, pre_val, act, grad_out, kernel, weight, margin, seams):
    channels = act.shape[-1]
    flat_grad = grad_out.reshape(-1, channels)
    d_weight = lax.dot_general(
        act.reshape(-1, channels),
        flat_grad,
        (((0,), (0,)), ((), ())),
        preferred_element_type=jnp.float32,
    )
    d_act = lax.dot_general(
        flat_grad, weight, (((1,), (1,)), ((), ())), preferred_element_type=jnp.float32
    ).reshape(pre_val.shape)
    logistic = jax.nn.sigmoid(pre_val)
    d_pre = d_act * logistic * (1.0 + pre_val * (1.0 - logistic))
    d_kernel, grad_wide = conv_back(widened, kernel, d_pre, margin)
    d_values = fold_back(grad_wide, margin, seams)
    grad_in = (grad_out.astype(jnp.float32) + d_values).astype(jnp.bfloat16)
    return (grad_in, d_kernel, d_weight)


def shards(fields, cotangent, kernel_one, weight_one, kernel_two, weight_two, seam_flags):
    batch_size, row_count, col_count, channels = fields.shape
    seams = seam_bits(seam_flags, col_count // COL_DEV)
    cells_all = (
        batch_size
        * row_count
        * col_count
        * lax.axis_size("strip")
        * lax.axis_size("blk")
        * lax.axis_size("dp")
    )
    factor = float(cells_all) ** (-0.5)
    wide_one = extend(fields, 1, seams).astype(jnp.float32)
    pre_one = depthwise(wide_one, kernel_one, 1, row_count)
    act_one = jax.nn.silu(pre_one).astype(jnp.bfloat16)
    hidden = (fields.astype(jnp.float32) + pointwise(act_one, weight_one)).astype(jnp.bfloat16)
    wide_two = extend(hidden, 2, seams).astype(jnp.float32)
    pre_two = depthwise(wide_two, kernel_two, 2, row_count)
    act_two = jax.nn.silu(pre_two).astype(jnp.bfloat16)
    grad_hidden, dk_two, dw_two = block_back(
        wide_two, pre_two, act_two, cotangent, kernel_two, weight_two, 2, seams
    )
    grad_fields, dk_one, dw_one = block_back(
        wide_one, pre_one, act_one, grad_hidden, kernel_one, weight_one, 1, seams
    )
    dk_one, dw_one, dk_two, dw_two = packed_sum(
        (dk_one, dw_one, dk_two, dw_two), ("strip", "blk", "dp"), tree_sum
    )
    return (grad_fields, dk_one * factor, dw_one * factor, dk_two * factor, dw_two * factor)


def solution(mesh):
    return jax.shard_map(
        shards,
        mesh=mesh,
        in_specs=(
            P("dp", "blk", "strip", None),
            P("dp", "blk", "strip", None),
            P(),
            P(),
            P(),
            P(),
            P(),
        ),
        out_specs=(P("dp", "blk", "strip", None), P(), P(), P(), P()),
        check_vma=False,
    )
```
